512 devices in a mesh: section: 2 (over core), tile: 256 (over z, y, x).
Axes of the slice: x: 4, y: 8, z: 8, core: 2. Of those that a mesh axis runs over, the one named last changes fastest.
Arguments:
- probe: bfloat16 [256, 2, 256], replicated, may hold values from -2.390625 to 2.390625
- kernel: bfloat16 [2, 256, 256], replicated, may hold values from -0.25 to 0.25
- object_slab: bfloat16 [4, 10240, 2, 256], P('section', 'tile'), as said below
- offsets: int32 [256], P('tile'), may hold values from 0 to 10239, as said below
- counts: int32 [256], P('tile'), may hold values from 1 to 1, as said below
- intensity: bfloat16 [256, 256, 256], P('tile'), may hold values from 0.5 to 3
Outputs:
- object_gradient: float32 [4, 10240, 2, 256], P('section', 'tile')
The draws below stay inside these ranges and needn't reach their ends.
Inputs may be any that keep to these rules, and one draw needn't show every extreme that they name: `object_slab`: real parts lie in 0.7 to 1.2 and imaginary parts in -0.4 to 0.4. offsets[q] - (q) * 40 lies in 0 to 39; it is 0 at the first slot, 39 at the last slot, and 39 at the first slot of some tile index other than 0. `counts`: every entry is 1; each tile index holds exactly one live scan position.
All inputs are finite; a program needn't handle non-finite values.
Results may differ from the reference program's by a relative error of at most 0.015.
Values may be sent and summed in bfloat16 or wider, within the bound.
No kernel may reach another device: no remote copies, remote signals or barrier semaphores. Data moves between devices by JAX's collectives and lax.ppermute only.
A program may use at most 64 MiB of HBM per device.

```python
import jax
import jax.numpy as jnp
from jax import lax

PROBE = 256
POS = 1
TR = 40
ROWS = 10240
SLICES = 4
POSITIONS = 256
TILES = 256


def draw_object_slab(key, part):
    key_real = jax.random.fold_in(key, 11)
    key_imag = jax.random.fold_in(key, 12)
    real_part = jax.random.uniform(key_real, (SLICES, ROWS, 1, PROBE), jnp.float32, 0.7, 1.2)
    imag_part = jax.random.uniform(key_imag, (SLICES, ROWS, 1, PROBE), jnp.float32, -0.4, 0.4)
    return jnp.concatenate((real_part, imag_part), axis=2).astype(jnp.bfloat16)


def draw_offsets(key, part):
    key_within = jax.random.fold_in(key, 31)
    key_far = jax.random.fold_in(key, 32)
    slot_ids = jnp.arange(POSITIONS, dtype=jnp.int32)
    within = jax.random.randint(key_within, (POSITIONS,), 0, TR, dtype=jnp.int32)
    far_tile = jax.random.randint(key_far, (), 1, TILES, dtype=jnp.int32)
    within = jnp.where(slot_ids == far_tile * POS, TR - 1, within)
    within = jnp.where(slot_ids == 0, 0, within)
    within = jnp.where(slot_ids == POSITIONS - 1, TR - 1, within)
    return (slot_ids // POS * TR + within).astype(jnp.int32)


def draw_counts(key, part):
    key_counts = jax.random.fold_in(key, 21)
    key_full = jax.random.fold_in(key, 22)
    drawn = jax.random.randint(key_counts, (TILES,), 1, POS + 1, dtype=jnp.int32)
    full_at = jax.random.randint(key_full, (), 0, TILES, dtype=jnp.int32)
    return jnp.where(jnp.arange(TILES, dtype=jnp.int32) == full_at, POS, drawn).astype(jnp.int32)


def steps_of(key, extent, cuts, least, top_value):
    def one(axis_at, blocks):
        heights = jax.random.uniform(jax.random.fold_in(jax.random.fold_in(key, 6), axis_at), (blocks,), jnp.float32, least / len(cuts), top_value / len(cuts))
        return jnp.repeat(jnp.exp(heights), extent[axis_at] // blocks).reshape((-1,) + (1,) * (len(extent) - axis_at - 1))

    gain = one(*cuts[0])
    for cut in cuts[1:]:
        gain = gain * one(*cut)
    return gain


def normal_values(key, shape, scale, bound, held_as=jnp.bfloat16):
    values = scale * jax.random.normal(key, shape, jnp.float32)
    return jnp.clip(values, min=-bound, max=bound).astype(held_as)


def setup_inputs(seed: int = 0) -> dict:
    seeds = jax.random.split(jax.random.key(seed), 7)
    return {
        "probe": normal_values(seeds[0], (PROBE, 2, PROBE), 0.4, 2.390625),
        "kernel": normal_values(seeds[1], (2, PROBE, PROBE), (2 * PROBE) ** -0.5, 0.25),
        "object_slab": draw_object_slab(jax.random.fold_in(seeds[6], 71), 0),
        "offsets": draw_offsets(jax.random.fold_in(seeds[6], 71), 0),
        "counts": draw_counts(jax.random.fold_in(seeds[6], 71), 0),
        "intensity": jnp.clip(0.5 + 2.5 * jax.random.uniform(seeds[5], (POSITIONS, PROBE, PROBE), jnp.float32) ** steps_of(seeds[5], (POSITIONS, PROBE, PROBE), ((0, 256),), -0.2, 0.2), 0.5, 3.0).astype(jnp.bfloat16),
    }


def dft_matrix(length):
    points = jnp.arange(length, dtype=jnp.int32)
    product_mod = points[:, None] * points[None, :] % length
    angle = 2.0 * 3.141592653589793 / length * product_mod.astype(jnp.float32)
    scale_fac = 1.0 / jnp.sqrt(jnp.float32(length))
    return jnp.stack((jnp.cos(angle) * scale_fac, -jnp.sin(angle) * scale_fac)).astype(jnp.bfloat16)

def product(form, first, second):
    return jnp.einsum(form, first.astype(jnp.float32), second.astype(jnp.float32), precision=lax.Precision.HIGHEST)

def apply_left(matrix, field):
    first_part = product('ij,...jck->...ick', matrix[0], field)
    second_part = product('ij,...jck->...ick', matrix[1], field)
    return jnp.stack((first_part[..., 0, :] - second_part[..., 1, :], first_part[..., 1, :] + second_part[..., 0, :]), axis=-2)

def apply_left_adj(matrix, field):
    first_part = product('ji,...jck->...ick', matrix[0], field)
    second_part = product('ji,...jck->...ick', matrix[1], field)
    return jnp.stack((first_part[..., 0, :] + second_part[..., 1, :], first_part[..., 1, :] - second_part[..., 0, :]), axis=-2)

def apply_right(field, matrix):
    first_part = product('...ick,lk->...icl', field, matrix[0])
    second_part = product('...ick,lk->...icl', field, matrix[1])
    return jnp.stack((first_part[..., 0, :] - second_part[..., 1, :], second_part[..., 0, :] + first_part[..., 1, :]), axis=-2)

def apply_right_conj(field, matrix):
    first_part = product('...ick,kl->...icl', field, matrix[0])
    second_part = product('...ick,kl->...icl', field, matrix[1])
    return jnp.stack((first_part[..., 0, :] + second_part[..., 1, :], first_part[..., 1, :] - second_part[..., 0, :]), axis=-2)

def complex_mul(first, second):
    first = first.astype(jnp.float32)
    second = second.astype(jnp.float32)
    return jnp.stack((first[..., 0, :] * second[..., 0, :] - first[..., 1, :] * second[..., 1, :], first[..., 0, :] * second[..., 1, :] + first[..., 1, :] * second[..., 0, :]), axis=-2)

def conj_mul(first, second):
    first = first.astype(jnp.float32)
    second = second.astype(jnp.float32)
    return jnp.stack((first[..., 0, :] * second[..., 0, :] + first[..., 1, :] * second[..., 1, :], first[..., 0, :] * second[..., 1, :] - first[..., 1, :] * second[..., 0, :]), axis=-2)

def reference(probe, kernel, object_slab, offsets, counts, intensity):
    width = probe.shape[0]
    dft_table = dft_matrix(width)
    doubled = jnp.concatenate((object_slab, object_slab[:, :width]), axis=1)
    slot_ids = jnp.arange(POSITIONS, dtype=jnp.int32)
    live_slots = (slot_ids % POS < jnp.repeat(counts, POS)).astype(jnp.float32)

    def one_position(carry, inputs):
        offset, alive, measured = inputs
        patches = lax.dynamic_slice_in_dim(doubled, offset, width, 1)
        field_now = probe
        incidents = []
        for slice_at in range(SLICES):
            incidents.append(field_now)
            phase = complex_mul(field_now, patches[slice_at]).astype(jnp.bfloat16)
            middle = apply_left(kernel, phase).astype(jnp.bfloat16)
            field_now = apply_right(middle, kernel).astype(jnp.bfloat16)
        half_far = apply_left(dft_table, field_now).astype(jnp.bfloat16)
        far = apply_right(half_far, dft_table)
        misfit = far[:, 0, :] ** 2 + far[:, 1, :] ** 2 - measured.astype(jnp.float32)
        grad_far = (far * misfit[:, None, :]).astype(jnp.bfloat16)
        half_back = apply_left_adj(dft_table, grad_far).astype(jnp.bfloat16)
        adjoint = apply_right_conj(half_back, dft_table).astype(jnp.bfloat16)
        gradients = []
        for slice_at in reversed(range(SLICES)):
            middle = apply_left_adj(kernel, adjoint).astype(jnp.bfloat16)
            phibar = apply_right_conj(middle, kernel)
            gradients.append(conj_mul(incidents[slice_at], phibar) * alive)
            adjoint = conj_mul(patches[slice_at], phibar).astype(jnp.bfloat16)
        gradients = jnp.stack(gradients[::-1])
        current = lax.dynamic_slice_in_dim(carry, offset, width, 1)
        carry = lax.dynamic_update_slice_in_dim(carry, current + gradients, offset, 1)
        return (carry, None)
    start_buf = jnp.zeros((SLICES, ROWS + width, 2, width), jnp.float32)
    buffer_all, _ = lax.scan(one_position, start_buf, (offsets, live_slots, intensity))
    head_rows = buffer_all[:, :width] + buffer_all[:, ROWS:]
    return jnp.concatenate((head_rows, buffer_all[:, width:ROWS]), axis=1)
```

```python
import jax
import jax.numpy as jnp
from jax import lax
from jax.sharding import PartitionSpec as P


def shifted(value, axis, steps):
    count = lax.axis_size(axis)
    pairs = [(source, (source + steps) % count) for source in range(count)]
    return lax.ppermute(value, axis, pairs)


def passed_along(shard, axis, by):
    length = lax.axis_size(axis)
    pairs = [(i, i + by) for i in range(length) if 0 <= i + by < length]
    return lax.ppermute(shard, axis, pairs)


def dft_matrix(length):
    points = jnp.arange(length, dtype=jnp.int32)
    product_mod = points[:, None] * points[None, :] % length
    angle = 2.0 * 3.141592653589793 / length * product_mod.astype(jnp.float32)
    scale_fac = 1.0 / jnp.sqrt(jnp.float32(length))
    return jnp.stack((jnp.cos(angle) * scale_fac, -jnp.sin(angle) * scale_fac)).astype(jnp.bfloat16)


def product(form, first, second):
    return jnp.einsum(form, first, second, preferred_element_type=jnp.float32)


def apply_left(matrix, field):
    first_part = product("ij,...jck->...ick", matrix[0], field)
    second_part = product("ij,...jck->...ick", matrix[1], field)
    return jnp.stack(
        (
            first_part[..., 0, :] - second_part[..., 1, :],
            first_part[..., 1, :] + second_part[..., 0, :],
        ),
        axis=-2,
    )


def apply_left_adj(matrix, field):
    first_part = product("ji,...jck->...ick", matrix[0], field)
    second_part = product("ji,...jck->...ick", matrix[1], field)
    return jnp.stack(
        (
            first_part[..., 0, :] + second_part[..., 1, :],
            first_part[..., 1, :] - second_part[..., 0, :],
        ),
        axis=-2,
    )


def apply_right(field, matrix):
    first_part = product("...ick,lk->...icl", field, matrix[0])
    second_part = product("...ick,lk->...icl", field, matrix[1])
    return jnp.stack(
        (
            first_part[..., 0, :] - second_part[..., 1, :],
            second_part[..., 0, :] + first_part[..., 1, :],
        ),
        axis=-2,
    )


def apply_right_conj(field, matrix):
    first_part = product("...ick,kl->...icl", field, matrix[0])
    second_part = product("...ick,kl->...icl", field, matrix[1])
    return jnp.stack(
        (
            first_part[..., 0, :] + second_part[..., 1, :],
            first_part[..., 1, :] - second_part[..., 0, :],
        ),
        axis=-2,
    )


def complex_mul(first, second):
    first = first.astype(jnp.float32)
    second = second.astype(jnp.float32)
    return jnp.stack(
        (
            first[..., 0, :] * second[..., 0, :] - first[..., 1, :] * second[..., 1, :],
            first[..., 0, :] * second[..., 1, :] + first[..., 1, :] * second[..., 0, :],
        ),
        axis=-2,
    )


def conj_mul(first, second):
    first = first.astype(jnp.float32)
    return jnp.stack(
        (
            first[..., 0, :] * second[..., 0, :] + first[..., 1, :] * second[..., 1, :],
            first[..., 0, :] * second[..., 1, :] - first[..., 1, :] * second[..., 0, :],
        ),
        axis=-2,
    )


def accumulate(gradients, starts, buffer_rows):
    slot_count, slice_count, width = (gradients.shape[0], gradients.shape[1], gradients.shape[-1])
    buffer_all = jnp.zeros((buffer_rows, slice_count, 2, width), jnp.float32)
    for slot_at in range(slot_count):
        start_row = starts[slot_at]
        current = lax.dynamic_slice_in_dim(buffer_all, start_row, width, 0)
        placed = jnp.transpose(gradients[slot_at], (1, 0, 2, 3))
        buffer_all = lax.dynamic_update_slice_in_dim(buffer_all, current + placed, start_row, 0)
    return buffer_all


def on_device(probe, kernel, object_slab, offsets, counts, intensity):
    width = probe.shape[0]
    slot_count = offsets.shape[0]
    local_rows = object_slab.shape[1]
    slice_count = object_slab.shape[0]
    sections = lax.axis_size("section")
    section_now = lax.axis_index("section")
    tile_now = lax.axis_index("tile")
    is_last = section_now == sections - 1
    dft_table = dft_matrix(width)
    reach = (local_rows + width - 2) // local_rows + 1
    blocks = [object_slab]
    for step_at in range(1, reach):
        blocks.append(shifted(blocks[-1], "tile", -1))
    window = jnp.concatenate(blocks, axis=1)
    relative = offsets - tile_now * local_rows
    patches = jax.vmap(lambda offset: lax.dynamic_slice_in_dim(window, offset, width, 1))(relative)
    live_slots = jnp.arange(slot_count, dtype=jnp.int32) < counts[0]

    def march(field_now, patches_here):
        incidents = []
        for slice_at in range(slice_count):
            incidents.append(field_now)
            phase = complex_mul(field_now, patches_here[..., slice_at, :, :, :]).astype(
                jnp.bfloat16
            )
            middle = apply_left(kernel, phase).astype(jnp.bfloat16)
            field_now = apply_right(middle, kernel).astype(jnp.bfloat16)
        return (field_now, jnp.stack(incidents, axis=-4))

    def far_adjoint(field_now, measured):
        half_far = apply_left(dft_table, field_now).astype(jnp.bfloat16)
        far = apply_right(half_far, dft_table)
        misfit = far[..., 0, :] ** 2 + far[..., 1, :] ** 2 - measured.astype(jnp.float32)
        grad_far = (far * misfit[..., None, :]).astype(jnp.bfloat16)
        half_back = apply_left_adj(dft_table, grad_far).astype(jnp.bfloat16)
        return apply_right_conj(half_back, dft_table).astype(jnp.bfloat16)

    def retreat(adjoint, patches_here, incidents):
        gradients = []
        for slice_at in reversed(range(slice_count)):
            middle = apply_left_adj(kernel, adjoint).astype(jnp.bfloat16)
            phibar = apply_right_conj(middle, kernel)
            gradients.append(conj_mul(incidents[..., slice_at, :, :, :], phibar))
            adjoint = conj_mul(patches_here[..., slice_at, :, :, :], phibar).astype(jnp.bfloat16)
        return (adjoint, jnp.stack(gradients[::-1], axis=-4))

    stored = jnp.zeros(patches.shape, jnp.bfloat16)
    gradients = jnp.zeros(patches.shape, jnp.float32)
    waves = jnp.broadcast_to(probe, (slot_count,) + probe.shape)
    for section_step in range(sections):
        if section_step > 0:
            waves = passed_along(waves, "section", 1)
        waves, stored = lax.cond(
            section_now == section_step,
            lambda field_in, kept: march(field_in, patches),
            lambda field_in, kept: (field_in, kept),
            waves,
            stored,
        )
    adjoints = lax.cond(
        is_last, lambda field_in: far_adjoint(field_in, intensity), lambda field_in: field_in, waves
    )
    for section_step in reversed(range(sections)):
        if section_step < sections - 1:
            adjoints = passed_along(adjoints, "section", -1)
        adjoints, gradients = lax.cond(
            section_now == section_step,
            lambda field_in, kept: retreat(field_in, patches, stored),
            lambda field_in, kept: (field_in, kept),
            adjoints,
            gradients,
        )
    gradients = gradients * live_slots.astype(jnp.float32)[:, None, None, None, None]
    nearby = accumulate(gradients, relative, reach * local_rows)
    own_rows = nearby[(reach - 1) * local_rows : reach * local_rows]
    for step_at in reversed(range(reach - 1)):
        block_rows = nearby[step_at * local_rows : (step_at + 1) * local_rows]
        own_rows = block_rows + shifted(own_rows.astype(jnp.bfloat16), "tile", 1).astype(
            block_rows.dtype
        )
    return jnp.transpose(own_rows, (1, 0, 2, 3))


def solution(mesh):
    return jax.shard_map(
        on_device,
        mesh=mesh,
        in_specs=(
            P(),
            P(),
            P("section", "tile", None, None),
            P("tile"),
            P("tile"),
            P("tile", None, None),
        ),
        out_specs=P("section", "tile", None, None),
        check_vma=False,
    )
```

```python
import functools

import jax
import jax.numpy as jnp
from jax import lax
from jax.sharding import PartitionSpec as P


def shifted(value, axis, steps):
    count = lax.axis_size(axis)
    pairs = [(source, (source + steps) % count) for source in range(count)]
    return lax.ppermute(value, axis, pairs)


def passed_along(shard, axis, by):
    length = lax.axis_size(axis)
    pairs = [(i, i + by) for i in range(length) if 0 <= i + by < length]
    return lax.ppermute(shard, axis, pairs)


def dft_matrix(length):
    points = jnp.arange(length, dtype=jnp.int32)
    product_mod = points[:, None] * points[None, :] % length
    angle = 2.0 * 3.141592653589793 / length * product_mod.astype(jnp.float32)
    scale_fac = 1.0 / jnp.sqrt(jnp.float32(length))
    return jnp.stack((jnp.cos(angle) * scale_fac, -jnp.sin(angle) * scale_fac)).astype(jnp.bfloat16)


def product(form, first, second):
    return jnp.einsum(form, first, second, preferred_element_type=jnp.float32)


def apply_left(matrix, field):
    first_part = product("ij,...jck->...ick", matrix[0], field)
    second_part = product("ij,...jck->...ick", matrix[1], field)
    return jnp.stack(
        (
            first_part[..., 0, :] - second_part[..., 1, :],
            first_part[..., 1, :] + second_part[..., 0, :],
        ),
        axis=-2,
    )


def apply_left_adj(matrix, field):
    first_part = product("ji,...jck->...ick", matrix[0], field)
    second_part = product("ji,...jck->...ick", matrix[1], field)
    return jnp.stack(
        (
            first_part[..., 0, :] + second_part[..., 1, :],
            first_part[..., 1, :] - second_part[..., 0, :],
        ),
        axis=-2,
    )


def apply_right(field, matrix):
    first_part = product("...ick,lk->...icl", field, matrix[0])
    second_part = product("...ick,lk->...icl", field, matrix[1])
    return jnp.stack(
        (
            first_part[..., 0, :] - second_part[..., 1, :],
            second_part[..., 0, :] + first_part[..., 1, :],
        ),
        axis=-2,
    )


def apply_right_conj(field, matrix):
    first_part = product("...ick,kl->...icl", field, matrix[0])
    second_part = product("...ick,kl->...icl", field, matrix[1])
    return jnp.stack(
        (
            first_part[..., 0, :] + second_part[..., 1, :],
            first_part[..., 1, :] - second_part[..., 0, :],
        ),
        axis=-2,
    )


def complex_mul(first, second):
    first = first.astype(jnp.float32)
    second = second.astype(jnp.float32)
    return jnp.stack(
        (
            first[..., 0, :] * second[..., 0, :] - first[..., 1, :] * second[..., 1, :],
            first[..., 0, :] * second[..., 1, :] + first[..., 1, :] * second[..., 0, :],
        ),
        axis=-2,
    )


def conj_mul(first, second):
    first = first.astype(jnp.float32)
    return jnp.stack(
        (
            first[..., 0, :] * second[..., 0, :] + first[..., 1, :] * second[..., 1, :],
            first[..., 0, :] * second[..., 1, :] - first[..., 1, :] * second[..., 0, :],
        ),
        axis=-2,
    )


def accumulate(gradients, starts, buffer_rows):
    slot_count, slice_count, width = (gradients.shape[0], gradients.shape[1], gradients.shape[-1])
    buffer_all = jnp.zeros((buffer_rows, slice_count, 2, width), jnp.float32)
    for slot_at in range(slot_count):
        start_row = starts[slot_at]
        current = lax.dynamic_slice_in_dim(buffer_all, start_row, width, 0)
        placed = jnp.transpose(gradients[slot_at], (1, 0, 2, 3))
        buffer_all = lax.dynamic_update_slice_in_dim(buffer_all, current + placed, start_row, 0)
    return buffer_all


def on_device(row_axis, tile_axes, probe, kernel, object_slab, offsets, counts, intensity):
    width = probe.shape[0]
    slot_count = offsets.shape[0]
    local_rows = object_slab.shape[1]
    slice_count = object_slab.shape[0]
    sections = lax.axis_size("section")
    section_now = lax.axis_index("section")
    row_size = lax.axis_size(row_axis)
    tile_count = lax.axis_size(tile_axes)
    tile_now = lax.axis_index(tile_axes)
    place = lax.axis_index(row_axis)
    is_last = section_now == sections - 1
    dft_table = dft_matrix(width)
    chunk_ids = jnp.arange(row_size, dtype=jnp.int32)
    later = [object_slab] + [
        lax.ppermute(
            object_slab,
            tile_axes,
            [(s, (s - ahead * row_size) % tile_count) for s in range(tile_count)],
        )
        for ahead in (1, 2)
    ]
    own_row = (chunk_ids <= place)[:, None, None, None, None, None]
    sent = jnp.where(
        own_row, jnp.stack(later[:2])[None], jnp.stack(later[1:])[None]
    )
    got = lax.all_to_all(sent, row_axis, 0, 0)
    got = lax.dynamic_slice_in_dim(jnp.concatenate((got, got), axis=0), place, row_size, 0)
    window = jnp.concatenate(
        [got[at % row_size, at // row_size] for at in range(2 * row_size)], axis=1
    )
    relative = offsets - tile_now * local_rows
    patches = jax.vmap(lambda offset: lax.dynamic_slice_in_dim(window, offset, width, 1))(relative)
    live_slots = jnp.arange(slot_count, dtype=jnp.int32) < counts[0]

    def march(field_now, patches_here):
        incidents = []
        for slice_at in range(slice_count):
            incidents.append(field_now)
            phase = complex_mul(field_now, patches_here[..., slice_at, :, :, :]).astype(
                jnp.bfloat16
            )
            middle = apply_left(kernel, phase).astype(jnp.bfloat16)
            field_now = apply_right(middle, kernel).astype(jnp.bfloat16)
        return (field_now, jnp.stack(incidents, axis=-4))

    def far_adjoint(field_now, measured):
        half_far = apply_left(dft_table, field_now).astype(jnp.bfloat16)
        far = apply_right(half_far, dft_table)
        misfit = far[..., 0, :] ** 2 + far[..., 1, :] ** 2 - measured.astype(jnp.float32)
        grad_far = (far * misfit[..., None, :]).astype(jnp.bfloat16)
        half_back = apply_left_adj(dft_table, grad_far).astype(jnp.bfloat16)
        return apply_right_conj(half_back, dft_table).astype(jnp.bfloat16)

    def retreat(adjoint, patches_here, incidents):
        gradients = []
        for slice_at in reversed(range(slice_count)):
            middle = apply_left_adj(kernel, adjoint).astype(jnp.bfloat16)
            phibar = apply_right_conj(middle, kernel)
            gradients.append(conj_mul(incidents[..., slice_at, :, :, :], phibar))
            adjoint = conj_mul(patches_here[..., slice_at, :, :, :], phibar).astype(jnp.bfloat16)
        return (adjoint, jnp.stack(gradients[::-1], axis=-4))

    stored = jnp.zeros(patches.shape, jnp.bfloat16)
    gradients = jnp.zeros(patches.shape, jnp.float32)
    waves = jnp.broadcast_to(probe, (slot_count,) + probe.shape)
    for section_step in range(sections):
        if section_step > 0:
            waves = passed_along(waves, "section", 1)
        waves, stored = lax.cond(
            section_now == section_step,
            lambda field_in, kept: march(field_in, patches),
            lambda field_in, kept: (field_in, kept),
            waves,
            stored,
        )
    adjoints = lax.cond(
        is_last, lambda field_in: far_adjoint(field_in, intensity), lambda field_in: field_in, waves
    )
    for section_step in reversed(range(sections)):
        if section_step < sections - 1:
            adjoints = passed_along(adjoints, "section", -1)
        adjoints, gradients = lax.cond(
            section_now == section_step,
            lambda field_in, kept: retreat(field_in, patches, stored),
            lambda field_in, kept: (field_in, kept),
            adjoints,
            gradients,
        )
    gradients = gradients * live_slots.astype(jnp.float32)[:, None, None, None, None]
    nearby = accumulate(gradients, offsets - tile_now * local_rows, 2 * row_size * local_rows)
    tiles = jnp.stack(
        [nearby[at * local_rows : (at + 1) * local_rows] for at in range(2 * row_size)], axis=0
    ).astype(jnp.bfloat16)
    tiles = tiles.reshape((2, row_size) + tiles.shape[1:]).swapaxes(0, 1)
    tiles = jnp.concatenate((tiles, tiles), axis=0)
    outgoing = lax.dynamic_slice_in_dim(tiles, row_size - place, row_size, 0)
    incoming = lax.all_to_all(outgoing, row_axis, 0, 0).astype(jnp.float32)
    same = (chunk_ids <= place)[:, None, None, None, None]
    first = incoming[:, 0]
    second = incoming[:, 1]
    own_rows = jnp.sum(jnp.where(same, first, 0.0), axis=0)
    spills = [
        jnp.sum(jnp.where(same, second, first), axis=0),
        jnp.sum(jnp.where(same, 0.0, second), axis=0),
    ]
    for ahead, spill in zip((1, 2), spills):
        own_rows = own_rows + lax.ppermute(
            spill.astype(jnp.bfloat16),
            tile_axes,
            [(s, (s + ahead * row_size) % tile_count) for s in range(tile_count)],
        ).astype(jnp.float32)
    return jnp.transpose(own_rows, (1, 0, 2, 3))


def row_length(devices):
    places = sorted({device.coords[0] for device in devices})
    return len(places)


def solution(mesh):
    sections, tiles = mesh.devices.shape
    row_size = row_length(list(mesh.devices[0]))
    grid = mesh.devices.reshape(sections, tiles // row_size, row_size)
    grid_mesh = jax.sharding.Mesh(grid, ("section", "lines", "x"))
    tile_axes = ("lines", "x")
    return jax.shard_map(
        functools.partial(on_device, "x", tile_axes),
        mesh=grid_mesh,
        in_specs=(
            P(),
            P(),
            P("section", tile_axes, None, None),
            P(tile_axes),
            P(tile_axes),
            P(tile_axes, None, None),
        ),
        out_specs=P("section", tile_axes, None, None),
        check_vma=False,
    )
```

```python
import functools

import jax
import jax.numpy as jnp
from jax import lax
from jax.sharding import PartitionSpec as P


def shifted(value, axis, steps):
    count = lax.axis_size(axis)
    pairs = [(source, (source + steps) % count) for source in range(count)]
    return lax.ppermute(value, axis, pairs)


def passed_along(shard, axis, by):
    length = lax.axis_size(axis)
    pairs = [(i, i + by) for i in range(length) if 0 <= i + by < length]
    return lax.ppermute(shard, axis, pairs)


def dft_matrix(length):
    points = jnp.arange(length, dtype=jnp.int32)
    product_mod = points[:, None] * points[None, :] % length
    angle = 2.0 * 3.141592653589793 / length * product_mod.astype(jnp.float32)
    scale_fac = 1.0 / jnp.sqrt(jnp.float32(length))
    return jnp.stack((jnp.cos(angle) * scale_fac, -jnp.sin(angle) * scale_fac)).astype(jnp.bfloat16)


def product(form, first, second):
    return jnp.einsum(form, first, second, preferred_element_type=jnp.float32)


def left_block(real, imag):
    top = jnp.stack((real, -imag), axis=-1)
    bottom = jnp.stack((imag, real), axis=-1)
    side = real.shape[0]
    return jnp.stack((top, bottom), axis=1).reshape(2 * side, 2 * side)


def right_block(real, imag):
    upper = jnp.stack((real, imag), axis=1)
    lower = jnp.stack((-imag, real), axis=1)
    side = real.shape[0]
    return jnp.stack((upper, lower), axis=0).reshape(2 * side, 2 * side)


def blocks_of(matrix):
    real, imag = matrix[0], matrix[1]
    return {
        "left": left_block(real, imag),
        "left_adj": left_block(real.T, -imag.T),
        "right": right_block(real.T, imag.T),
        "right_conj": right_block(real, -imag),
    }


def apply_left(block, field):
    lead = field.shape[:-3]
    rows, parts, width = field.shape[-3:]
    flat = field.reshape(lead + (rows * parts, width))
    return product("ab,...bk->...ak", block, flat).reshape(field.shape)


def apply_right(field, block):
    lead = field.shape[:-3]
    rows, parts, width = field.shape[-3:]
    flat = field.reshape(lead + (rows, parts * width))
    return product("...ia,ab->...ib", flat, block).reshape(field.shape)


def complex_mul(first, second):
    first = first.astype(jnp.float32)
    second = second.astype(jnp.float32)
    return jnp.stack(
        (
            first[..., 0, :] * second[..., 0, :] - first[..., 1, :] * second[..., 1, :],
            first[..., 0, :] * second[..., 1, :] + first[..., 1, :] * second[..., 0, :],
        ),
        axis=-2,
    )


def conj_mul(first, second):
    first = first.astype(jnp.float32)
    return jnp.stack(
        (
            first[..., 0, :] * second[..., 0, :] + first[..., 1, :] * second[..., 1, :],
            first[..., 0, :] * second[..., 1, :] - first[..., 1, :] * second[..., 0, :],
        ),
        axis=-2,
    )


def accumulate(gradients, starts, buffer_rows):
    width = gradients.shape[-1]
    margin = buffer_rows - width
    placed = jnp.transpose(gradients[0], (1, 0, 2, 3))
    padded = jnp.pad(placed, ((margin, margin), (0, 0), (0, 0), (0, 0)))
    return lax.dynamic_slice_in_dim(padded, margin - starts[0], buffer_rows, 0)


def on_device(row_axis, tile_axes, probe, kernel, object_slab, offsets, counts, intensity):
    width = probe.shape[0]
    slot_count = offsets.shape[0]
    local_rows = object_slab.shape[1]
    slice_count = object_slab.shape[0]
    sections = lax.axis_size("section")
    section_now = lax.axis_index("section")
    row_size = lax.axis_size(row_axis)
    tile_count = lax.axis_size(tile_axes)
    tile_now = lax.axis_index(tile_axes)
    place = lax.axis_index(row_axis)
    is_last = section_now == sections - 1
    dft_table = blocks_of(dft_matrix(width))
    kernel = blocks_of(kernel)
    chunk_ids = jnp.arange(row_size, dtype=jnp.int32)
    later = [object_slab] + [
        lax.ppermute(
            object_slab,
            tile_axes,
            [(s, (s - ahead * row_size) % tile_count) for s in range(tile_count)],
        )
        for ahead in (1, 2)
    ]
    own_row = (chunk_ids <= place)[:, None, None, None, None, None]
    sent = jnp.where(
        own_row, jnp.stack(later[:2])[None], jnp.stack(later[1:])[None]
    )
    got = lax.all_to_all(sent, row_axis, 0, 0)
    got = lax.dynamic_slice_in_dim(jnp.concatenate((got, got), axis=0), place, row_size, 0)
    window = jnp.concatenate(
        [got[at % row_size, at // row_size] for at in range(2 * row_size)], axis=1
    )
    relative = offsets - tile_now * local_rows
    patches = jax.vmap(lambda offset: lax.dynamic_slice_in_dim(window, offset, width, 1))(relative)
    live_slots = jnp.arange(slot_count, dtype=jnp.int32) < counts[0]

    def march(field_now, patches_here):
        incidents = []
        for slice_at in range(slice_count):
            incidents.append(field_now)
            phase = complex_mul(field_now, patches_here[..., slice_at, :, :, :]).astype(
                jnp.bfloat16
            )
            middle = apply_left(kernel["left"], phase).astype(jnp.bfloat16)
            field_now = apply_right(middle, kernel["right"]).astype(jnp.bfloat16)
        return (field_now, jnp.stack(incidents, axis=-4))

    def far_adjoint(field_now, measured):
        half_far = apply_left(dft_table["left"], field_now).astype(jnp.bfloat16)
        far = apply_right(half_far, dft_table["right"])
        misfit = far[..., 0, :] ** 2 + far[..., 1, :] ** 2 - measured.astype(jnp.float32)
        grad_far = (far * misfit[..., None, :]).astype(jnp.bfloat16)
        half_back = apply_left(dft_table["left_adj"], grad_far).astype(jnp.bfloat16)
        return apply_right(half_back, dft_table["right_conj"]).astype(jnp.bfloat16)

    def retreat(adjoint, patches_here, incidents):
        gradients = []
        for slice_at in reversed(range(slice_count)):
            middle = apply_left(kernel["left_adj"], adjoint).astype(jnp.bfloat16)
            phibar = apply_right(middle, kernel["right_conj"])
            gradients.append(conj_mul(incidents[..., slice_at, :, :, :], phibar))
            adjoint = conj_mul(patches_here[..., slice_at, :, :, :], phibar).astype(jnp.bfloat16)
        return (adjoint, jnp.stack(gradients[::-1], axis=-4))

    stored = jnp.zeros(patches.shape, jnp.bfloat16)
    gradients = jnp.zeros(patches.shape, jnp.float32)
    waves = jnp.broadcast_to(probe, (slot_count,) + probe.shape)
    for section_step in range(sections):
        if section_step > 0:
            waves = passed_along(waves, "section", 1)
        waves, stored = lax.cond(
            section_now == section_step,
            lambda field_in, kept: march(field_in, patches),
            lambda field_in, kept: (field_in, kept),
            waves,
            stored,
        )
    adjoints = lax.cond(
        is_last, lambda field_in: far_adjoint(field_in, intensity), lambda field_in: field_in, waves
    )
    for section_step in reversed(range(sections)):
        if section_step < sections - 1:
            adjoints = passed_along(adjoints, "section", -1)
        adjoints, gradients = lax.cond(
            section_now == section_step,
            lambda field_in, kept: retreat(field_in, patches, stored),
            lambda field_in, kept: (field_in, kept),
            adjoints,
            gradients,
        )
    gradients = gradients * live_slots.astype(jnp.float32)[:, None, None, None, None]
    nearby = accumulate(gradients, offsets - tile_now * local_rows, 2 * row_size * local_rows)
    tiles = jnp.stack(
        [nearby[at * local_rows : (at + 1) * local_rows] for at in range(2 * row_size)], axis=0
    ).astype(jnp.bfloat16)
    tiles = tiles.reshape((2, row_size) + tiles.shape[1:]).swapaxes(0, 1)
    tiles = jnp.concatenate((tiles, tiles), axis=0)
    outgoing = lax.dynamic_slice_in_dim(tiles, row_size - place, row_size, 0)
    incoming = lax.all_to_all(outgoing, row_axis, 0, 0).astype(jnp.float32)
    same = (chunk_ids <= place)[:, None, None, None, None]
    first = incoming[:, 0]
    second = incoming[:, 1]
    own_rows = jnp.sum(jnp.where(same, first, 0.0), axis=0)
    spills = [
        jnp.sum(jnp.where(same, second, first), axis=0),
        jnp.sum(jnp.where(same, 0.0, second), axis=0),
    ]
    for ahead, spill in zip((1, 2), spills):
        own_rows = own_rows + lax.ppermute(
            spill.astype(jnp.bfloat16),
            tile_axes,
            [(s, (s + ahead * row_size) % tile_count) for s in range(tile_count)],
        ).astype(jnp.float32)
    return jnp.transpose(own_rows, (1, 0, 2, 3))


def row_length(devices):
    places = sorted({device.coords[0] for device in devices})
    return len(places)


def solution(mesh):
    sections, tiles = mesh.devices.shape
    row_size = row_length(list(mesh.devices[0]))
    grid = mesh.devices.reshape(sections, tiles // row_size, row_size)
    grid_mesh = jax.sharding.Mesh(grid, ("section", "lines", "x"))
    tile_axes = ("lines", "x")
    return jax.shard_map(
        functools.partial(on_device, "x", tile_axes),
        mesh=grid_mesh,
        in_specs=(
            P(),
            P(),
            P("section", tile_axes, None, None),
            P(tile_axes),
            P(tile_axes),
            P(tile_axes, None, None),
        ),
        out_specs=P("section", tile_axes, None, None),
        check_vma=False,
    )
```

```python
import functools

import jax
from jax.experimental import pallas as pl
import jax.numpy as jnp
from jax import lax
from jax.sharding import PartitionSpec as P


def shifted(value, axis, steps):
    count = lax.axis_size(axis)
    pairs = [(source, (source + steps) % count) for source in range(count)]
    return lax.ppermute(value, axis, pairs)


def passed_along(shard, axis, by):
    length = lax.axis_size(axis)
    pairs = [(i, i + by) for i in range(length) if 0 <= i + by < length]
    return lax.ppermute(shard, axis, pairs)


def dft_matrix(length):
    points = jnp.arange(length, dtype=jnp.int32)
    product_mod = points[:, None] * points[None, :] % length
    angle = 2.0 * 3.141592653589793 / length * product_mod.astype(jnp.float32)
    scale_fac = 1.0 / jnp.sqrt(jnp.float32(length))
    return jnp.stack((jnp.cos(angle) * scale_fac, -jnp.sin(angle) * scale_fac)).astype(jnp.bfloat16)


def product(form, first, second):
    return jnp.einsum(form, first, second, preferred_element_type=jnp.float32)


def apply_left(matrix, field):
    first_part = product("ij,...jck->...ick", matrix[0], field)
    second_part = product("ij,...jck->...ick", matrix[1], field)
    return jnp.stack(
        (
            first_part[..., 0, :] - second_part[..., 1, :],
            first_part[..., 1, :] + second_part[..., 0, :],
        ),
        axis=-2,
    )


def apply_left_adj(matrix, field):
    first_part = product("ji,...jck->...ick", matrix[0], field)
    second_part = product("ji,...jck->...ick", matrix[1], field)
    return jnp.stack(
        (
            first_part[..., 0, :] + second_part[..., 1, :],
            first_part[..., 1, :] - second_part[..., 0, :],
        ),
        axis=-2,
    )


def apply_right(field, matrix):
    first_part = product("...ick,lk->...icl", field, matrix[0])
    second_part = product("...ick,lk->...icl", field, matrix[1])
    return jnp.stack(
        (
            first_part[..., 0, :] - second_part[..., 1, :],
            second_part[..., 0, :] + first_part[..., 1, :],
        ),
        axis=-2,
    )


def apply_right_conj(field, matrix):
    first_part = product("...ick,kl->...icl", field, matrix[0])
    second_part = product("...ick,kl->...icl", field, matrix[1])
    return jnp.stack(
        (
            first_part[..., 0, :] + second_part[..., 1, :],
            first_part[..., 1, :] - second_part[..., 0, :],
        ),
        axis=-2,
    )


def complex_mul(first, second):
    first = first.astype(jnp.float32)
    second = second.astype(jnp.float32)
    return jnp.stack(
        (
            first[..., 0, :] * second[..., 0, :] - first[..., 1, :] * second[..., 1, :],
            first[..., 0, :] * second[..., 1, :] + first[..., 1, :] * second[..., 0, :],
        ),
        axis=-2,
    )


def conj_mul(first, second):
    first = first.astype(jnp.float32)
    return jnp.stack(
        (
            first[..., 0, :] * second[..., 0, :] + first[..., 1, :] * second[..., 1, :],
            first[..., 0, :] * second[..., 1, :] - first[..., 1, :] * second[..., 0, :],
        ),
        axis=-2,
    )


def accumulate(gradients, starts, buffer_rows):
    width = gradients.shape[-1]
    margin = buffer_rows - width
    placed = jnp.transpose(gradients[0], (1, 0, 2, 3))
    padded = jnp.pad(placed, ((margin, margin), (0, 0), (0, 0), (0, 0)))
    return lax.dynamic_slice_in_dim(padded, margin - starts[0], buffer_rows, 0)


def real_dot(first, second):
    return jnp.dot(first, second, preferred_element_type=jnp.float32)


def times_left(real, imag, field_real, field_imag):
    return (
        real_dot(real, field_real) - real_dot(imag, field_imag),
        real_dot(real, field_imag) + real_dot(imag, field_real),
    )


def times_left_adj(real_t, imag_t, field_real, field_imag):
    return (
        real_dot(real_t, field_real) + real_dot(imag_t, field_imag),
        real_dot(real_t, field_imag) - real_dot(imag_t, field_real),
    )


def times_right(field_real, field_imag, real_t, imag_t):
    return (
        real_dot(field_real, real_t) - real_dot(field_imag, imag_t),
        real_dot(field_real, imag_t) + real_dot(field_imag, real_t),
    )


def times_right_conj(field_real, field_imag, real, imag):
    return (
        real_dot(field_real, real) + real_dot(field_imag, imag),
        real_dot(field_imag, real) - real_dot(field_real, imag),
    )


def rounded(pair):
    return (pair[0].astype(jnp.bfloat16), pair[1].astype(jnp.bfloat16))


def march_kernel(field_ref, patch_ref, mat_ref, out_ref, incident_ref):
    real, imag, real_t, imag_t = mat_ref[0], mat_ref[1], mat_ref[2], mat_ref[3]
    field_real, field_imag = field_ref[0], field_ref[1]
    for slice_at in range(patch_ref.shape[0]):
        incident_ref[slice_at, 0] = field_real
        incident_ref[slice_at, 1] = field_imag
        first_real = field_real.astype(jnp.float32)
        first_imag = field_imag.astype(jnp.float32)
        second_real = patch_ref[slice_at, 0].astype(jnp.float32)
        second_imag = patch_ref[slice_at, 1].astype(jnp.float32)
        phase = rounded(
            (
                first_real * second_real - first_imag * second_imag,
                first_real * second_imag + first_imag * second_real,
            )
        )
        middle = rounded(times_left(real, imag, *phase))
        field_real, field_imag = rounded(times_right(*middle, real_t, imag_t))
    out_ref[0] = field_real
    out_ref[1] = field_imag


def far_kernel(field_ref, measured_ref, mat_ref, out_ref):
    real, imag, real_t, imag_t = mat_ref[0], mat_ref[1], mat_ref[2], mat_ref[3]
    half_far = rounded(times_left(real, imag, field_ref[0], field_ref[1]))
    far_real, far_imag = times_right(*half_far, real_t, imag_t)
    misfit = far_real * far_real + far_imag * far_imag - measured_ref[...].astype(jnp.float32)
    grad_far = rounded((far_real * misfit, far_imag * misfit))
    half_back = rounded(times_left_adj(real_t, imag_t, *grad_far))
    back_real, back_imag = rounded(times_right_conj(*half_back, real, imag))
    out_ref[0] = back_real
    out_ref[1] = back_imag


def retreat_kernel(back_ref, patch_ref, incident_ref, mat_ref, out_ref, grad_ref):
    real, imag, real_t, imag_t = mat_ref[0], mat_ref[1], mat_ref[2], mat_ref[3]
    back = (back_ref[0], back_ref[1])
    for slice_at in reversed(range(patch_ref.shape[0])):
        middle = rounded(times_left_adj(real_t, imag_t, *back))
        bar_real, bar_imag = times_right_conj(*middle, real, imag)
        inc_real = incident_ref[slice_at, 0].astype(jnp.float32)
        inc_imag = incident_ref[slice_at, 1].astype(jnp.float32)
        grad_ref[slice_at, 0] = inc_real * bar_real + inc_imag * bar_imag
        grad_ref[slice_at, 1] = inc_real * bar_imag - inc_imag * bar_real
        pat_real = patch_ref[slice_at, 0].astype(jnp.float32)
        pat_imag = patch_ref[slice_at, 1].astype(jnp.float32)
        back = rounded(
            (pat_real * bar_real + pat_imag * bar_imag, pat_real * bar_imag - pat_imag * bar_real)
        )
    out_ref[0] = back[0]
    out_ref[1] = back[1]


def planes_of(matrix):
    return jnp.stack((matrix[0], matrix[1], matrix[0].T, matrix[1].T))


def run_kernel(body, outs, flops, *args):
    moved = sum(arg.size * arg.dtype.itemsize for arg in args)
    listed = outs if isinstance(outs, tuple) else (outs,)
    moved += sum(out.size * jnp.dtype(out.dtype).itemsize for out in listed)
    return pl.pallas_call(
        body,
        out_shape=outs,
        cost_estimate=pl.CostEstimate(flops=flops, transcendentals=0, bytes_accessed=moved),
    )(*args)


def on_device(row_axis, tile_axes, probe, kernel, object_slab, offsets, counts, intensity):
    width = probe.shape[0]
    slot_count = offsets.shape[0]
    local_rows = object_slab.shape[1]
    slice_count = object_slab.shape[0]
    sections = lax.axis_size("section")
    section_now = lax.axis_index("section")
    row_size = lax.axis_size(row_axis)
    tile_count = lax.axis_size(tile_axes)
    tile_now = lax.axis_index(tile_axes)
    place = lax.axis_index(row_axis)
    is_last = section_now == sections - 1
    dft_table = dft_matrix(width)
    chunk_ids = jnp.arange(row_size, dtype=jnp.int32)
    later = [object_slab] + [
        lax.ppermute(
            object_slab,
            tile_axes,
            [(s, (s - ahead * row_size) % tile_count) for s in range(tile_count)],
        )
        for ahead in (1, 2)
    ]
    own_row = (chunk_ids <= place)[:, None, None, None, None, None]
    sent = jnp.where(
        own_row, jnp.stack(later[:2])[None], jnp.stack(later[1:])[None]
    )
    got = lax.all_to_all(sent, row_axis, 0, 0)
    got = lax.dynamic_slice_in_dim(jnp.concatenate((got, got), axis=0), place, row_size, 0)
    window = jnp.concatenate(
        [got[at % row_size, at // row_size] for at in range(2 * row_size)], axis=1
    )
    relative = offsets - tile_now * local_rows
    patches = jax.vmap(lambda offset: lax.dynamic_slice_in_dim(window, offset, width, 1))(relative)
    live_slots = jnp.arange(slot_count, dtype=jnp.int32) < counts[0]

    planes = jnp.transpose(patches[0], (0, 2, 1, 3))
    kernel_planes = planes_of(kernel)
    dft_planes = planes_of(dft_matrix(width))
    field_shape = jax.ShapeDtypeStruct((2, width, width), jnp.bfloat16)
    dot_flops = 2 * width**3

    def march(field_in):
        outs = (field_shape, jax.ShapeDtypeStruct(planes.shape, jnp.bfloat16))
        flops = slice_count * 8 * dot_flops
        return tuple(run_kernel(march_kernel, outs, flops, field_in, planes, kernel_planes))

    def far_adjoint(field_in):
        return run_kernel(far_kernel, field_shape, 16 * dot_flops, field_in, intensity[0], dft_planes)

    def retreat(back_in, incidents):
        outs = (field_shape, jax.ShapeDtypeStruct(planes.shape, jnp.float32))
        flops = slice_count * 8 * dot_flops
        return tuple(
            run_kernel(retreat_kernel, outs, flops, back_in, planes, incidents, kernel_planes)
        )

    stored = jnp.zeros(planes.shape, jnp.bfloat16)
    gradients = jnp.zeros(planes.shape, jnp.float32)
    waves = jnp.transpose(probe, (1, 0, 2))
    for section_step in range(sections):
        if section_step > 0:
            waves = passed_along(waves, "section", 1)
        waves, stored = lax.cond(
            section_now == section_step,
            lambda field_in, kept: march(field_in),
            lambda field_in, kept: (field_in, kept),
            waves,
            stored,
        )
    adjoints = lax.cond(
        is_last, lambda field_in: far_adjoint(field_in), lambda field_in: field_in, waves
    )
    for section_step in reversed(range(sections)):
        if section_step < sections - 1:
            adjoints = passed_along(adjoints, "section", -1)
        adjoints, gradients = lax.cond(
            section_now == section_step,
            lambda field_in, kept: retreat(field_in, stored),
            lambda field_in, kept: (field_in, kept),
            adjoints,
            gradients,
        )
    gradients = jnp.transpose(gradients, (0, 2, 1, 3))[None]
    gradients = gradients * live_slots.astype(jnp.float32)[:, None, None, None, None]
    nearby = accumulate(gradients, offsets - tile_now * local_rows, 2 * row_size * local_rows)
    tiles = jnp.stack(
        [nearby[at * local_rows : (at + 1) * local_rows] for at in range(2 * row_size)], axis=0
    ).astype(jnp.bfloat16)
    tiles = tiles.reshape((2, row_size) + tiles.shape[1:]).swapaxes(0, 1)
    tiles = jnp.concatenate((tiles, tiles), axis=0)
    outgoing = lax.dynamic_slice_in_dim(tiles, row_size - place, row_size, 0)
    incoming = lax.all_to_all(outgoing, row_axis, 0, 0).astype(jnp.float32)
    same = (chunk_ids <= place)[:, None, None, None, None]
    first = incoming[:, 0]
    second = incoming[:, 1]
    own_rows = jnp.sum(jnp.where(same, first, 0.0), axis=0)
    spills = [
        jnp.sum(jnp.where(same, second, first), axis=0),
        jnp.sum(jnp.where(same, 0.0, second), axis=0),
    ]
    for ahead, spill in zip((1, 2), spills):
        own_rows = own_rows + lax.ppermute(
            spill.astype(jnp.bfloat16),
            tile_axes,
            [(s, (s + ahead * row_size) % tile_count) for s in range(tile_count)],
        ).astype(jnp.float32)
    return jnp.transpose(own_rows, (1, 0, 2, 3))


def row_length(devices):
    places = sorted({device.coords[0] for device in devices})
    return len(places)


def solution(mesh):
    sections, tiles = mesh.devices.shape
    row_size = row_length(list(mesh.devices[0]))
    grid = mesh.devices.reshape(sections, tiles // row_size, row_size)
    grid_mesh = jax.sharding.Mesh(grid, ("section", "lines", "x"))
    tile_axes = ("lines", "x")
    return jax.shard_map(
        functools.partial(on_device, "x", tile_axes),
        mesh=grid_mesh,
        in_specs=(
            P(),
            P(),
            P("section", tile_axes, None, None),
            P(tile_axes),
            P(tile_axes),
            P(tile_axes, None, None),
        ),
        out_specs=P("section", tile_axes, None, None),
        check_vma=False,
    )
```

```python
import functools

import jax
from jax.experimental import pallas as pl
import jax.numpy as jnp
from jax import lax
from jax.sharding import PartitionSpec as P


def shifted(value, axis, steps):
    count = lax.axis_size(axis)
    pairs = [(source, (source + steps) % count) for source in range(count)]
    return lax.ppermute(value, axis, pairs)


def passed_along(shard, axis, by):
    length = lax.axis_size(axis)
    pairs = [(i, i + by) for i in range(length) if 0 <= i + by < length]
    return lax.ppermute(shard, axis, pairs)


def dft_matrix(length):
    points = jnp.arange(length, dtype=jnp.int32)
    product_mod = points[:, None] * points[None, :] % length
    angle = 2.0 * 3.141592653589793 / length * product_mod.astype(jnp.float32)
    scale_fac = 1.0 / jnp.sqrt(jnp.float32(length))
    return jnp.stack((jnp.cos(angle) * scale_fac, -jnp.sin(angle) * scale_fac)).astype(jnp.bfloat16)


def product(form, first, second):
    return jnp.einsum(form, first, second, preferred_element_type=jnp.float32)


def apply_left(matrix, field):
    first_part = product("ij,...jck->...ick", matrix[0], field)
    second_part = product("ij,...jck->...ick", matrix[1], field)
    return jnp.stack(
        (
            first_part[..., 0, :] - second_part[..., 1, :],
            first_part[..., 1, :] + second_part[..., 0, :],
        ),
        axis=-2,
    )


def apply_left_adj(matrix, field):
    first_part = product("ji,...jck->...ick", matrix[0], field)
    second_part = product("ji,...jck->...ick", matrix[1], field)
    return jnp.stack(
        (
            first_part[..., 0, :] + second_part[..., 1, :],
            first_part[..., 1, :] - second_part[..., 0, :],
        ),
        axis=-2,
    )


def apply_right(field, matrix):
    first_part = product("...ick,lk->...icl", field, matrix[0])
    second_part = product("...ick,lk->...icl", field, matrix[1])
    return jnp.stack(
        (
            first_part[..., 0, :] - second_part[..., 1, :],
            second_part[..., 0, :] + first_part[..., 1, :],
        ),
        axis=-2,
    )


def apply_right_conj(field, matrix):
    first_part = product("...ick,kl->...icl", field, matrix[0])
    second_part = product("...ick,kl->...icl", field, matrix[1])
    return jnp.stack(
        (
            first_part[..., 0, :] + second_part[..., 1, :],
            first_part[..., 1, :] - second_part[..., 0, :],
        ),
        axis=-2,
    )


def complex_mul(first, second):
    first = first.astype(jnp.float32)
    second = second.astype(jnp.float32)
    return jnp.stack(
        (
            first[..., 0, :] * second[..., 0, :] - first[..., 1, :] * second[..., 1, :],
            first[..., 0, :] * second[..., 1, :] + first[..., 1, :] * second[..., 0, :],
        ),
        axis=-2,
    )


def conj_mul(first, second):
    first = first.astype(jnp.float32)
    return jnp.stack(
        (
            first[..., 0, :] * second[..., 0, :] + first[..., 1, :] * second[..., 1, :],
            first[..., 0, :] * second[..., 1, :] - first[..., 1, :] * second[..., 0, :],
        ),
        axis=-2,
    )


def accumulate(gradients, starts, buffer_rows):
    width = gradients.shape[-1]
    margin = buffer_rows - width
    placed = jnp.transpose(gradients[0], (1, 0, 2, 3))
    padded = jnp.pad(placed, ((margin, margin), (0, 0), (0, 0), (0, 0)))
    return lax.dynamic_slice_in_dim(padded, margin - starts[0], buffer_rows, 0)


def real_dot(first, second):
    return jnp.dot(first, second, preferred_element_type=jnp.float32)


def times_left(real, imag, field_real, field_imag):
    return (
        real_dot(real, field_real) - real_dot(imag, field_imag),
        real_dot(real, field_imag) + real_dot(imag, field_real),
    )


def times_left_adj(real_t, imag_t, field_real, field_imag):
    return (
        real_dot(real_t, field_real) + real_dot(imag_t, field_imag),
        real_dot(real_t, field_imag) - real_dot(imag_t, field_real),
    )


def times_right(field_real, field_imag, real_t, imag_t):
    return (
        real_dot(field_real, real_t) - real_dot(field_imag, imag_t),
        real_dot(field_real, imag_t) + real_dot(field_imag, real_t),
    )


def times_right_conj(field_real, field_imag, real, imag):
    return (
        real_dot(field_real, real) + real_dot(field_imag, imag),
        real_dot(field_imag, real) - real_dot(field_real, imag),
    )


def rounded(pair):
    return (pair[0].astype(jnp.bfloat16), pair[1].astype(jnp.bfloat16))


def march_kernel(field_ref, patch_ref, mat_ref, out_ref, incident_ref):
    real, imag, real_t, imag_t = mat_ref[0], mat_ref[1], mat_ref[2], mat_ref[3]
    field_real, field_imag = field_ref[0], field_ref[1]
    for slice_at in range(patch_ref.shape[0]):
        incident_ref[slice_at, 0] = field_real
        incident_ref[slice_at, 1] = field_imag
        first_real = field_real.astype(jnp.float32)
        first_imag = field_imag.astype(jnp.float32)
        second_real = patch_ref[slice_at, 0].astype(jnp.float32)
        second_imag = patch_ref[slice_at, 1].astype(jnp.float32)
        phase = rounded(
            (
                first_real * second_real - first_imag * second_imag,
                first_real * second_imag + first_imag * second_real,
            )
        )
        middle = rounded(times_left(real, imag, *phase))
        field_real, field_imag = rounded(times_right(*middle, real_t, imag_t))
    out_ref[0] = field_real
    out_ref[1] = field_imag


def far_kernel(field_ref, measured_ref, mat_ref, out_ref):
    real, imag, real_t, imag_t = mat_ref[0], mat_ref[1], mat_ref[2], mat_ref[3]
    half_far = rounded(times_left(real, imag, field_ref[0], field_ref[1]))
    far_real, far_imag = times_right(*half_far, real_t, imag_t)
    misfit = far_real * far_real + far_imag * far_imag - measured_ref[...].astype(jnp.float32)
    grad_far = rounded((far_real * misfit, far_imag * misfit))
    half_back = rounded(times_left_adj(real_t, imag_t, *grad_far))
    back_real, back_imag = rounded(times_right_conj(*half_back, real, imag))
    out_ref[0] = back_real
    out_ref[1] = back_imag


def retreat_kernel(back_ref, patch_ref, incident_ref, mat_ref, out_ref, grad_ref):
    real, imag, real_t, imag_t = mat_ref[0], mat_ref[1], mat_ref[2], mat_ref[3]
    back = (back_ref[0], back_ref[1])
    for slice_at in reversed(range(patch_ref.shape[0])):
        middle = rounded(times_left_adj(real_t, imag_t, *back))
        bar_real, bar_imag = times_right_conj(*middle, real, imag)
        inc_real = incident_ref[slice_at, 0].astype(jnp.float32)
        inc_imag = incident_ref[slice_at, 1].astype(jnp.float32)
        grad_ref[slice_at, 0] = inc_real * bar_real + inc_imag * bar_imag
        grad_ref[slice_at, 1] = inc_real * bar_imag - inc_imag * bar_real
        pat_real = patch_ref[slice_at, 0].astype(jnp.float32)
        pat_imag = patch_ref[slice_at, 1].astype(jnp.float32)
        back = rounded(
            (pat_real * bar_real + pat_imag * bar_imag, pat_real * bar_imag - pat_imag * bar_real)
        )
    out_ref[0] = back[0]
    out_ref[1] = back[1]


def planes_of(matrix):
    return jnp.stack((matrix[0], matrix[1], matrix[0].T, matrix[1].T))


def run_kernel(body, outs, flops, *args):
    moved = sum(arg.size * arg.dtype.itemsize for arg in args)
    listed = outs if isinstance(outs, tuple) else (outs,)
    moved += sum(out.size * jnp.dtype(out.dtype).itemsize for out in listed)
    return pl.pallas_call(
        body,
        out_shape=outs,
        cost_estimate=pl.CostEstimate(flops=flops, transcendentals=0, bytes_accessed=moved),
    )(*args)


def on_device(row_axis, tile_axes, probe, kernel, object_slab, offsets, counts, intensity):
    width = probe.shape[0]
    slot_count = offsets.shape[0]
    local_rows = object_slab.shape[1]
    slice_count = object_slab.shape[0]
    sections = lax.axis_size("section")
    section_now = lax.axis_index("section")
    row_size = lax.axis_size(row_axis)
    tile_count = lax.axis_size(tile_axes)
    tile_now = lax.axis_index(tile_axes)
    place = lax.axis_index(row_axis)
    is_last = section_now == sections - 1
    dft_table = dft_matrix(width)
    chunk_ids = jnp.arange(row_size, dtype=jnp.int32)
    later = [object_slab] + [
        lax.ppermute(
            object_slab,
            tile_axes,
            [(s, (s - ahead * row_size) % tile_count) for s in range(tile_count)],
        )
        for ahead in (1, 2)
    ]
    own_row = (chunk_ids <= place)[:, None, None, None, None, None]
    sent = jnp.where(
        own_row, jnp.stack(later[:2])[None], jnp.stack(later[1:])[None]
    )
    got = lax.all_to_all(sent, row_axis, 0, 0)
    got = lax.dynamic_slice_in_dim(jnp.concatenate((got, got), axis=0), place, row_size, 0)
    window = jnp.concatenate(
        [got[at % row_size, at // row_size] for at in range(2 * row_size)], axis=1
    )
    relative = offsets - tile_now * local_rows
    patches = jax.vmap(lambda offset: lax.dynamic_slice_in_dim(window, offset, width, 1))(relative)
    live_slots = jnp.arange(slot_count, dtype=jnp.int32) < counts[0]

    planes = jnp.transpose(patches[0], (0, 2, 1, 3))
    kernel_planes = planes_of(kernel)
    dft_planes = planes_of(dft_matrix(width))
    field_shape = jax.ShapeDtypeStruct((2, width, width), jnp.bfloat16)
    dot_flops = 2 * width**3

    def march(field_in):
        outs = (field_shape, jax.ShapeDtypeStruct(planes.shape, jnp.bfloat16))
        flops = planes.shape[0] * 8 * dot_flops
        return tuple(run_kernel(march_kernel, outs, flops, field_in, planes, kernel_planes))

    def far_adjoint(field_in):
        return run_kernel(far_kernel, field_shape, 16 * dot_flops, field_in, intensity[0], dft_planes)

    def retreat(back_in, incidents):
        outs = (field_shape, jax.ShapeDtypeStruct(planes.shape, jnp.float32))
        flops = planes.shape[0] * 8 * dot_flops
        return tuple(
            run_kernel(retreat_kernel, outs, flops, back_in, planes, incidents, kernel_planes)
        )

    other = lax.ppermute(planes, "section", [(at, sections - 1 - at) for at in range(sections)])
    both = jnp.concatenate((planes, other, planes), axis=0)
    planes = lax.dynamic_slice_in_dim(both, section_now * slice_count, sections * slice_count, 0)
    waves = jnp.transpose(probe, (1, 0, 2))
    waves, stored = march(waves)
    adjoints = far_adjoint(waves)
    adjoints, gradients = retreat(adjoints, stored)
    gradients = lax.dynamic_slice_in_dim(gradients, section_now * slice_count, slice_count, 0)
    gradients = jnp.transpose(gradients, (0, 2, 1, 3))[None]
    gradients = gradients * live_slots.astype(jnp.float32)[:, None, None, None, None]
    nearby = accumulate(gradients, offsets - tile_now * local_rows, 2 * row_size * local_rows)
    tiles = jnp.stack(
        [nearby[at * local_rows : (at + 1) * local_rows] for at in range(2 * row_size)], axis=0
    ).astype(jnp.bfloat16)
    tiles = tiles.reshape((2, row_size) + tiles.shape[1:]).swapaxes(0, 1)
    tiles = jnp.concatenate((tiles, tiles), axis=0)
    outgoing = lax.dynamic_slice_in_dim(tiles, row_size - place, row_size, 0)
    incoming = lax.all_to_all(outgoing, row_axis, 0, 0).astype(jnp.float32)
    same = (chunk_ids <= place)[:, None, None, None, None]
    first = incoming[:, 0]
    second = incoming[:, 1]
    own_rows = jnp.sum(jnp.where(same, first, 0.0), axis=0)
    spills = [
        jnp.sum(jnp.where(same, second, first), axis=0),
        jnp.sum(jnp.where(same, 0.0, second), axis=0),
    ]
    for ahead, spill in zip((1, 2), spills):
        own_rows = own_rows + lax.ppermute(
            spill.astype(jnp.bfloat16),
            tile_axes,
            [(s, (s + ahead * row_size) % tile_count) for s in range(tile_count)],
        ).astype(jnp.float32)
    return jnp.transpose(own_rows, (1, 0, 2, 3))


def row_length(devices):
    places = sorted({device.coords[0] for device in devices})
    return len(places)


def solution(mesh):
    sections, tiles = mesh.devices.shape
    row_size = row_length(list(mesh.devices[0]))
    grid = mesh.devices.reshape(sections, tiles // row_size, row_size)
    grid_mesh = jax.sharding.Mesh(grid, ("section", "lines", "x"))
    tile_axes = ("lines", "x")
    return jax.shard_map(
        functools.partial(on_device, "x", tile_axes),
        mesh=grid_mesh,
        in_specs=(
            P(),
            P(),
            P("section", tile_axes, None, None),
            P(tile_axes),
            P(tile_axes),
            P(tile_axes, None, None),
        ),
        out_specs=P("section", tile_axes, None, None),
        check_vma=False,
    )
```

```python
import functools

import jax
import ml_dtypes
import numpy as np
from jax.experimental import pallas as pl
import jax.numpy as jnp
from jax import lax
from jax.sharding import PartitionSpec as P


def shifted(value, axis, steps):
    count = lax.axis_size(axis)
    pairs = [(source, (source + steps) % count) for source in range(count)]
    return lax.ppermute(value, axis, pairs)


def passed_along(shard, axis, by):
    length = lax.axis_size(axis)
    pairs = [(i, i + by) for i in range(length) if 0 <= i + by < length]
    return lax.ppermute(shard, axis, pairs)


def dft_matrix(length):
    points = jnp.arange(length, dtype=jnp.int32)
    product_mod = points[:, None] * points[None, :] % length
    angle = 2.0 * 3.141592653589793 / length * product_mod.astype(jnp.float32)
    scale_fac = 1.0 / jnp.sqrt(jnp.float32(length))
    return jnp.stack((jnp.cos(angle) * scale_fac, -jnp.sin(angle) * scale_fac)).astype(jnp.bfloat16)


def product(form, first, second):
    return jnp.einsum(form, first, second, preferred_element_type=jnp.float32)


def apply_left(matrix, field):
    first_part = product("ij,...jck->...ick", matrix[0], field)
    second_part = product("ij,...jck->...ick", matrix[1], field)
    return jnp.stack(
        (
            first_part[..., 0, :] - second_part[..., 1, :],
            first_part[..., 1, :] + second_part[..., 0, :],
        ),
        axis=-2,
    )


def apply_left_adj(matrix, field):
    first_part = product("ji,...jck->...ick", matrix[0], field)
    second_part = product("ji,...jck->...ick", matrix[1], field)
    return jnp.stack(
        (
            first_part[..., 0, :] + second_part[..., 1, :],
            first_part[..., 1, :] - second_part[..., 0, :],
        ),
        axis=-2,
    )


def apply_right(field, matrix):
    first_part = product("...ick,lk->...icl", field, matrix[0])
    second_part = product("...ick,lk->...icl", field, matrix[1])
    return jnp.stack(
        (
            first_part[..., 0, :] - second_part[..., 1, :],
            second_part[..., 0, :] + first_part[..., 1, :],
        ),
        axis=-2,
    )


def apply_right_conj(field, matrix):
    first_part = product("...ick,kl->...icl", field, matrix[0])
    second_part = product("...ick,kl->...icl", field, matrix[1])
    return jnp.stack(
        (
            first_part[..., 0, :] + second_part[..., 1, :],
            first_part[..., 1, :] - second_part[..., 0, :],
        ),
        axis=-2,
    )


def complex_mul(first, second):
    first = first.astype(jnp.float32)
    second = second.astype(jnp.float32)
    return jnp.stack(
        (
            first[..., 0, :] * second[..., 0, :] - first[..., 1, :] * second[..., 1, :],
            first[..., 0, :] * second[..., 1, :] + first[..., 1, :] * second[..., 0, :],
        ),
        axis=-2,
    )


def conj_mul(first, second):
    first = first.astype(jnp.float32)
    return jnp.stack(
        (
            first[..., 0, :] * second[..., 0, :] + first[..., 1, :] * second[..., 1, :],
            first[..., 0, :] * second[..., 1, :] - first[..., 1, :] * second[..., 0, :],
        ),
        axis=-2,
    )


def accumulate(gradients, starts, buffer_rows):
    width = gradients.shape[-1]
    margin = buffer_rows - width
    placed = jnp.transpose(gradients[0], (1, 0, 2, 3))
    padded = jnp.pad(placed, ((margin, margin), (0, 0), (0, 0), (0, 0)))
    return lax.dynamic_slice_in_dim(padded, margin - starts[0], buffer_rows, 0)


def real_dot(first, second):
    return jnp.dot(first, second, preferred_element_type=jnp.float32)


def times_left(real, imag, field_real, field_imag):
    return (
        real_dot(real, field_real) - real_dot(imag, field_imag),
        real_dot(real, field_imag) + real_dot(imag, field_real),
    )


def times_left_adj(real_t, imag_t, field_real, field_imag):
    return (
        real_dot(real_t, field_real) + real_dot(imag_t, field_imag),
        real_dot(real_t, field_imag) - real_dot(imag_t, field_real),
    )


def times_right(field_real, field_imag, real_t, imag_t):
    return (
        real_dot(field_real, real_t) - real_dot(field_imag, imag_t),
        real_dot(field_real, imag_t) + real_dot(field_imag, real_t),
    )


def times_right_conj(field_real, field_imag, real, imag):
    return (
        real_dot(field_real, real) + real_dot(field_imag, imag),
        real_dot(field_imag, real) - real_dot(field_real, imag),
    )


def rounded(pair):
    return (pair[0].astype(jnp.bfloat16), pair[1].astype(jnp.bfloat16))


def march_kernel(field_ref, patch_ref, mat_ref, out_ref, incident_ref):
    real, imag, real_t, imag_t = mat_ref[0], mat_ref[1], mat_ref[2], mat_ref[3]
    field_real, field_imag = field_ref[0], field_ref[1]
    for slice_at in range(patch_ref.shape[0]):
        incident_ref[slice_at, 0] = field_real
        incident_ref[slice_at, 1] = field_imag
        first_real = field_real.astype(jnp.float32)
        first_imag = field_imag.astype(jnp.float32)
        second_real = patch_ref[slice_at, 0].astype(jnp.float32)
        second_imag = patch_ref[slice_at, 1].astype(jnp.float32)
        phase = rounded(
            (
                first_real * second_real - first_imag * second_imag,
                first_real * second_imag + first_imag * second_real,
            )
        )
        middle = rounded(times_left(real, imag, *phase))
        field_real, field_imag = rounded(times_right(*middle, real_t, imag_t))
    out_ref[0] = field_real
    out_ref[1] = field_imag


def far_kernel(field_ref, measured_ref, mat_ref, out_ref):
    real, imag, real_t, imag_t = mat_ref[0], mat_ref[1], mat_ref[2], mat_ref[3]
    half_far = rounded(times_left(real, imag, field_ref[0], field_ref[1]))
    far_real, far_imag = times_right(*half_far, real_t, imag_t)
    misfit = far_real * far_real + far_imag * far_imag - measured_ref[...].astype(jnp.float32)
    grad_far = rounded((far_real * misfit, far_imag * misfit))
    half_back = rounded(times_left_adj(real_t, imag_t, *grad_far))
    back_real, back_imag = rounded(times_right_conj(*half_back, real, imag))
    out_ref[0] = back_real
    out_ref[1] = back_imag


def retreat_kernel(back_ref, patch_ref, incident_ref, mat_ref, out_ref, grad_ref):
    real, imag, real_t, imag_t = mat_ref[0], mat_ref[1], mat_ref[2], mat_ref[3]
    back = (back_ref[0], back_ref[1])
    for slice_at in reversed(range(patch_ref.shape[0])):
        middle = rounded(times_left_adj(real_t, imag_t, *back))
        bar_real, bar_imag = times_right_conj(*middle, real, imag)
        inc_real = incident_ref[slice_at, 0].astype(jnp.float32)
        inc_imag = incident_ref[slice_at, 1].astype(jnp.float32)
        grad_ref[slice_at, 0] = inc_real * bar_real + inc_imag * bar_imag
        grad_ref[slice_at, 1] = inc_real * bar_imag - inc_imag * bar_real
        pat_real = patch_ref[slice_at, 0].astype(jnp.float32)
        pat_imag = patch_ref[slice_at, 1].astype(jnp.float32)
        back = rounded(
            (pat_real * bar_real + pat_imag * bar_imag, pat_real * bar_imag - pat_imag * bar_real)
        )
    out_ref[0] = back[0]
    out_ref[1] = back[1]


def planes_of(matrix):
    return jnp.stack((matrix[0], matrix[1], matrix[0].T, matrix[1].T))


def dft_planes_of(length):
    points = np.arange(length)
    angle = 2.0 * np.pi * (np.outer(points, points) % length) / length
    real = np.cos(angle) / np.sqrt(length)
    imag = -np.sin(angle) / np.sqrt(length)
    table = np.stack((real, imag, real.T, imag.T)).astype(ml_dtypes.bfloat16)
    return jnp.asarray(table)


def run_kernel(body, outs, flops, *args):
    moved = sum(arg.size * arg.dtype.itemsize for arg in args)
    listed = outs if isinstance(outs, tuple) else (outs,)
    moved += sum(out.size * jnp.dtype(out.dtype).itemsize for out in listed)
    return pl.pallas_call(
        body,
        out_shape=outs,
        cost_estimate=pl.CostEstimate(flops=flops, transcendentals=0, bytes_accessed=moved),
    )(*args)


def on_device(row_axis, tile_axes, probe, kernel, object_slab, offsets, counts, intensity):
    width = probe.shape[0]
    slot_count = offsets.shape[0]
    local_rows = object_slab.shape[1]
    slice_count = object_slab.shape[0]
    sections = lax.axis_size("section")
    section_now = lax.axis_index("section")
    row_size = lax.axis_size(row_axis)
    tile_count = lax.axis_size(tile_axes)
    tile_now = lax.axis_index(tile_axes)
    place = lax.axis_index(row_axis)
    is_last = section_now == sections - 1
    dft_table = dft_matrix(width)
    chunk_ids = jnp.arange(row_size, dtype=jnp.int32)
    later = [object_slab] + [
        lax.ppermute(
            object_slab,
            tile_axes,
            [(s, (s - ahead * row_size) % tile_count) for s in range(tile_count)],
        )
        for ahead in (1, 2)
    ]
    own_row = (chunk_ids <= place)[:, None, None, None, None, None]
    sent = jnp.where(
        own_row, jnp.stack(later[:2])[None], jnp.stack(later[1:])[None]
    )
    got = lax.all_to_all(sent, row_axis, 0, 0)
    got = lax.dynamic_slice_in_dim(jnp.concatenate((got, got), axis=0), place, row_size, 0)
    window = jnp.concatenate(
        [got[at % row_size, at // row_size] for at in range(2 * row_size)], axis=1
    )
    relative = offsets - tile_now * local_rows
    patches = jax.vmap(lambda offset: lax.dynamic_slice_in_dim(window, offset, width, 1))(relative)
    live_slots = jnp.arange(slot_count, dtype=jnp.int32) < counts[0]

    planes = jnp.transpose(patches[0], (0, 2, 1, 3))
    kernel_planes = planes_of(kernel)
    dft_planes = dft_planes_of(width)
    field_shape = jax.ShapeDtypeStruct((2, width, width), jnp.bfloat16)
    dot_flops = 2 * width**3

    def march(field_in):
        outs = (field_shape, jax.ShapeDtypeStruct(planes.shape, jnp.bfloat16))
        flops = slice_count * 8 * dot_flops
        return tuple(run_kernel(march_kernel, outs, flops, field_in, planes, kernel_planes))

    def far_adjoint(field_in):
        return run_kernel(far_kernel, field_shape, 16 * dot_flops, field_in, intensity[0], dft_planes)

    def retreat(back_in, incidents):
        outs = (field_shape, jax.ShapeDtypeStruct(planes.shape, jnp.float32))
        flops = slice_count * 8 * dot_flops
        return tuple(
            run_kernel(retreat_kernel, outs, flops, back_in, planes, incidents, kernel_planes)
        )

    first_section = section_now == 0
    waves, early = march(jnp.transpose(probe, (1, 0, 2)))
    waves, late = march(passed_along(waves, "section", 1))
    stored = jnp.where(first_section, early, late)
    adjoints, late = retreat(far_adjoint(waves), stored)
    adjoints, early = retreat(passed_along(adjoints, "section", -1), stored)
    gradients = jnp.where(first_section, early, late)
    gradients = jnp.transpose(gradients, (0, 2, 1, 3))[None]
    gradients = gradients * live_slots.astype(jnp.float32)[:, None, None, None, None]
    nearby = accumulate(gradients, offsets - tile_now * local_rows, 2 * row_size * local_rows)
    tiles = jnp.stack(
        [nearby[at * local_rows : (at + 1) * local_rows] for at in range(2 * row_size)], axis=0
    ).astype(jnp.bfloat16)
    tiles = tiles.reshape((2, row_size) + tiles.shape[1:]).swapaxes(0, 1)
    tiles = jnp.concatenate((tiles, tiles), axis=0)
    outgoing = lax.dynamic_slice_in_dim(tiles, row_size - place, row_size, 0)
    incoming = lax.all_to_all(outgoing, row_axis, 0, 0).astype(jnp.float32)
    same = (chunk_ids <= place)[:, None, None, None, None]
    first = incoming[:, 0]
    second = incoming[:, 1]
    own_rows = jnp.sum(jnp.where(same, first, 0.0), axis=0)
    spills = [
        jnp.sum(jnp.where(same, second, first), axis=0),
        jnp.sum(jnp.where(same, 0.0, second), axis=0),
    ]
    for ahead, spill in zip((1, 2), spills):
        own_rows = own_rows + lax.ppermute(
            spill.astype(jnp.bfloat16),
            tile_axes,
            [(s, (s + ahead * row_size) % tile_count) for s in range(tile_count)],
        ).astype(jnp.float32)
    return jnp.transpose(own_rows, (1, 0, 2, 3))


def row_length(devices):
    places = sorted({device.coords[0] for device in devices})
    return len(places)


def solution(mesh):
    sections, tiles = mesh.devices.shape
    row_size = row_length(list(mesh.devices[0]))
    grid = mesh.devices.reshape(sections, tiles // row_size, row_size)
    grid_mesh = jax.sharding.Mesh(grid, ("section", "lines", "x"))
    tile_axes = ("lines", "x")
    return jax.shard_map(
        functools.partial(on_device, "x", tile_axes),
        mesh=grid_mesh,
        in_specs=(
            P(),
            P(),
            P("section", tile_axes, None, None),
            P(tile_axes),
            P(tile_axes),
            P(tile_axes, None, None),
        ),
        out_specs=P("section", tile_axes, None, None),
        check_vma=False,
    )
```

```python
import functools

import jax
from jax.experimental import pallas as pl
import jax.numpy as jnp
from jax import lax
from jax.sharding import PartitionSpec as P


def shifted(value, axis, steps):
    count = lax.axis_size(axis)
    pairs = [(source, (source + steps) % count) for source in range(count)]
    return lax.ppermute(value, axis, pairs)


def passed_along(shard, axis, by):
    length = lax.axis_size(axis)
    pairs = [(i, i + by) for i in range(length) if 0 <= i + by < length]
    return lax.ppermute(shard, axis, pairs)


def dft_matrix(length):
    points = jnp.arange(length, dtype=jnp.int32)
    product_mod = points[:, None] * points[None, :] % length
    angle = 2.0 * 3.141592653589793 / length * product_mod.astype(jnp.float32)
    scale_fac = 1.0 / jnp.sqrt(jnp.float32(length))
    return jnp.stack((jnp.cos(angle) * scale_fac, -jnp.sin(angle) * scale_fac)).astype(jnp.bfloat16)


def product(form, first, second):
    return jnp.einsum(form, first, second, preferred_element_type=jnp.float32)


def apply_left(matrix, field):
    first_part = product("ij,...jck->...ick", matrix[0], field)
    second_part = product("ij,...jck->...ick", matrix[1], field)
    return jnp.stack(
        (
            first_part[..., 0, :] - second_part[..., 1, :],
            first_part[..., 1, :] + second_part[..., 0, :],
        ),
        axis=-2,
    )


def apply_left_adj(matrix, field):
    first_part = product("ji,...jck->...ick", matrix[0], field)
    second_part = product("ji,...jck->...ick", matrix[1], field)
    return jnp.stack(
        (
            first_part[..., 0, :] + second_part[..., 1, :],
            first_part[..., 1, :] - second_part[..., 0, :],
        ),
        axis=-2,
    )


def apply_right(field, matrix):
    first_part = product("...ick,lk->...icl", field, matrix[0])
    second_part = product("...ick,lk->...icl", field, matrix[1])
    return jnp.stack(
        (
            first_part[..., 0, :] - second_part[..., 1, :],
            second_part[..., 0, :] + first_part[..., 1, :],
        ),
        axis=-2,
    )


def apply_right_conj(field, matrix):
    first_part = product("...ick,kl->...icl", field, matrix[0])
    second_part = product("...ick,kl->...icl", field, matrix[1])
    return jnp.stack(
        (
            first_part[..., 0, :] + second_part[..., 1, :],
            first_part[..., 1, :] - second_part[..., 0, :],
        ),
        axis=-2,
    )


def complex_mul(first, second):
    first = first.astype(jnp.float32)
    second = second.astype(jnp.float32)
    return jnp.stack(
        (
            first[..., 0, :] * second[..., 0, :] - first[..., 1, :] * second[..., 1, :],
            first[..., 0, :] * second[..., 1, :] + first[..., 1, :] * second[..., 0, :],
        ),
        axis=-2,
    )


def conj_mul(first, second):
    first = first.astype(jnp.float32)
    return jnp.stack(
        (
            first[..., 0, :] * second[..., 0, :] + first[..., 1, :] * second[..., 1, :],
            first[..., 0, :] * second[..., 1, :] - first[..., 1, :] * second[..., 0, :],
        ),
        axis=-2,
    )


def accumulate(gradients, starts, buffer_rows):
    width = gradients.shape[-1]
    margin = buffer_rows - width
    placed = jnp.transpose(gradients[0], (1, 0, 2, 3))
    padded = jnp.pad(placed, ((margin, margin), (0, 0), (0, 0), (0, 0)))
    return lax.dynamic_slice_in_dim(padded, margin - starts[0], buffer_rows, 0)


def real_dot(first, second):
    return jnp.dot(first, second, preferred_element_type=jnp.float32)


def times_left(real, imag, field_real, field_imag):
    return (
        real_dot(real, field_real) - real_dot(imag, field_imag),
        real_dot(real, field_imag) + real_dot(imag, field_real),
    )


def times_left_adj(real_t, imag_t, field_real, field_imag):
    return (
        real_dot(real_t, field_real) + real_dot(imag_t, field_imag),
        real_dot(real_t, field_imag) - real_dot(imag_t, field_real),
    )


def times_right(field_real, field_imag, real_t, imag_t):
    return (
        real_dot(field_real, real_t) - real_dot(field_imag, imag_t),
        real_dot(field_real, imag_t) + real_dot(field_imag, real_t),
    )


def times_right_conj(field_real, field_imag, real, imag):
    return (
        real_dot(field_real, real) + real_dot(field_imag, imag),
        real_dot(field_imag, real) - real_dot(field_real, imag),
    )


def rounded(pair):
    return (pair[0].astype(jnp.bfloat16), pair[1].astype(jnp.bfloat16))


def march_steps(field, patch_ref, mats, incident_ref):
    real, imag, real_t, imag_t = mats
    field_real, field_imag = field
    for slice_at in range(patch_ref.shape[0]):
        incident_ref[slice_at, 0] = field_real
        incident_ref[slice_at, 1] = field_imag
        first_real = field_real.astype(jnp.float32)
        first_imag = field_imag.astype(jnp.float32)
        second_real = patch_ref[slice_at, 0].astype(jnp.float32)
        second_imag = patch_ref[slice_at, 1].astype(jnp.float32)
        phase = rounded(
            (
                first_real * second_real - first_imag * second_imag,
                first_real * second_imag + first_imag * second_real,
            )
        )
        middle = rounded(times_left(real, imag, *phase))
        field_real, field_imag = rounded(times_right(*middle, real_t, imag_t))
    return (field_real, field_imag)


def far_steps(field, measured, mats):
    real, imag, real_t, imag_t = mats
    half_far = rounded(times_left(real, imag, *field))
    far_real, far_imag = times_right(*half_far, real_t, imag_t)
    misfit = far_real * far_real + far_imag * far_imag - measured.astype(jnp.float32)
    grad_far = rounded((far_real * misfit, far_imag * misfit))
    half_back = rounded(times_left_adj(real_t, imag_t, *grad_far))
    return rounded(times_right_conj(*half_back, real, imag))


def retreat_steps(back, patch_ref, incident_ref, mats, grad_ref):
    real, imag, real_t, imag_t = mats
    for slice_at in reversed(range(patch_ref.shape[0])):
        middle = rounded(times_left_adj(real_t, imag_t, *back))
        bar_real, bar_imag = times_right_conj(*middle, real, imag)
        inc_real = incident_ref[slice_at, 0].astype(jnp.float32)
        inc_imag = incident_ref[slice_at, 1].astype(jnp.float32)
        grad_ref[slice_at, 0] = inc_real * bar_real + inc_imag * bar_imag
        grad_ref[slice_at, 1] = inc_real * bar_imag - inc_imag * bar_real
        pat_real = patch_ref[slice_at, 0].astype(jnp.float32)
        pat_imag = patch_ref[slice_at, 1].astype(jnp.float32)
        back = rounded(
            (pat_real * bar_real + pat_imag * bar_imag, pat_real * bar_imag - pat_imag * bar_real)
        )
    return back


def mats_of(mat_ref):
    return (mat_ref[0], mat_ref[1], mat_ref[2], mat_ref[3])


def march_kernel(field_ref, patch_ref, mat_ref, out_ref, incident_ref):
    field = march_steps((field_ref[0], field_ref[1]), patch_ref, mats_of(mat_ref), incident_ref)
    out_ref[0] = field[0]
    out_ref[1] = field[1]


def middle_kernel(
    field_ref, patch_ref, mat_ref, measured_ref, dft_ref, out_ref, grad_ref, incident_ref
):
    mats = mats_of(mat_ref)
    field = march_steps((field_ref[0], field_ref[1]), patch_ref, mats, incident_ref)
    back = far_steps(field, measured_ref[...], mats_of(dft_ref))
    back = retreat_steps(back, patch_ref, incident_ref, mats, grad_ref)
    out_ref[0] = back[0]
    out_ref[1] = back[1]


def retreat_kernel(back_ref, patch_ref, incident_ref, mat_ref, out_ref, grad_ref):
    back = retreat_steps(
        (back_ref[0], back_ref[1]), patch_ref, incident_ref, mats_of(mat_ref), grad_ref
    )
    out_ref[0] = back[0]
    out_ref[1] = back[1]


def planes_of(matrix):
    return jnp.stack((matrix[0], matrix[1], matrix[0].T, matrix[1].T))


def run_kernel(body, outs, flops, *args):
    moved = sum(arg.size * arg.dtype.itemsize for arg in args)
    listed = outs if isinstance(outs, tuple) else (outs,)
    moved += sum(out.size * jnp.dtype(out.dtype).itemsize for out in listed)
    return pl.pallas_call(
        body,
        out_shape=outs,
        cost_estimate=pl.CostEstimate(flops=flops, transcendentals=0, bytes_accessed=moved),
    )(*args)


def on_device(row_axis, tile_axes, probe, kernel, object_slab, offsets, counts, intensity):
    width = probe.shape[0]
    slot_count = offsets.shape[0]
    local_rows = object_slab.shape[1]
    slice_count = object_slab.shape[0]
    sections = lax.axis_size("section")
    section_now = lax.axis_index("section")
    row_size = lax.axis_size(row_axis)
    tile_count = lax.axis_size(tile_axes)
    tile_now = lax.axis_index(tile_axes)
    place = lax.axis_index(row_axis)
    is_last = section_now == sections - 1
    dft_table = dft_matrix(width)
    chunk_ids = jnp.arange(row_size, dtype=jnp.int32)
    later = [object_slab] + [
        lax.ppermute(
            object_slab,
            tile_axes,
            [(s, (s - ahead * row_size) % tile_count) for s in range(tile_count)],
        )
        for ahead in (1, 2)
    ]
    own_row = (chunk_ids <= place)[:, None, None, None, None, None]
    sent = jnp.where(
        own_row, jnp.stack(later[:2])[None], jnp.stack(later[1:])[None]
    )
    got = lax.all_to_all(sent, row_axis, 0, 0)
    got = lax.dynamic_slice_in_dim(jnp.concatenate((got, got), axis=0), place, row_size, 0)
    window = jnp.concatenate(
        [got[at % row_size, at // row_size] for at in range(2 * row_size)], axis=1
    )
    relative = offsets - tile_now * local_rows
    patches = jax.vmap(lambda offset: lax.dynamic_slice_in_dim(window, offset, width, 1))(relative)
    live_slots = jnp.arange(slot_count, dtype=jnp.int32) < counts[0]

    planes = jnp.transpose(patches[0], (0, 2, 1, 3))
    kernel_planes = planes_of(kernel)
    dft_planes = planes_of(dft_matrix(width))
    field_shape = jax.ShapeDtypeStruct((2, width, width), jnp.bfloat16)
    dot_flops = 2 * width**3

    def march(field_in):
        outs = (field_shape, jax.ShapeDtypeStruct(planes.shape, jnp.bfloat16))
        flops = slice_count * 8 * dot_flops
        return tuple(run_kernel(march_kernel, outs, flops, field_in, planes, kernel_planes))

    def retreat(back_in, incidents):
        outs = (field_shape, jax.ShapeDtypeStruct(planes.shape, jnp.float32))
        flops = slice_count * 8 * dot_flops
        return tuple(
            run_kernel(retreat_kernel, outs, flops, back_in, planes, incidents, kernel_planes)
        )

    def whole(field_in):
        outs = (
            field_shape,
            jax.ShapeDtypeStruct(planes.shape, jnp.float32),
            jax.ShapeDtypeStruct(planes.shape, jnp.bfloat16),
        )
        flops = slice_count * 16 * dot_flops + 16 * dot_flops
        back, grads, _ = run_kernel(
            middle_kernel, outs, flops, field_in, planes, kernel_planes, intensity[0], dft_planes
        )
        return (back, grads)

    stored = jnp.zeros(planes.shape, jnp.bfloat16)
    gradients = jnp.zeros(planes.shape, jnp.float32)
    waves = jnp.transpose(probe, (1, 0, 2))
    for section_step in range(sections - 1):
        if section_step > 0:
            waves = passed_along(waves, "section", 1)
        waves, stored = lax.cond(
            section_now == section_step,
            lambda field_in, kept: march(field_in),
            lambda field_in, kept: (field_in, kept),
            waves,
            stored,
        )
    waves = passed_along(waves, "section", 1)
    adjoints, gradients = lax.cond(
        is_last,
        lambda field_in, kept: whole(field_in),
        lambda field_in, kept: (field_in, kept),
        waves,
        gradients,
    )
    for section_step in reversed(range(sections - 1)):
        adjoints = passed_along(adjoints, "section", -1)
        adjoints, gradients = lax.cond(
            section_now == section_step,
            lambda field_in, kept: retreat(field_in, stored),
            lambda field_in, kept: (field_in, kept),
            adjoints,
            gradients,
        )
    gradients = jnp.transpose(gradients, (0, 2, 1, 3))[None]
    gradients = gradients * live_slots.astype(jnp.float32)[:, None, None, None, None]
    nearby = accumulate(gradients, offsets - tile_now * local_rows, 2 * row_size * local_rows)
    tiles = jnp.stack(
        [nearby[at * local_rows : (at + 1) * local_rows] for at in range(2 * row_size)], axis=0
    ).astype(jnp.bfloat16)
    tiles = tiles.reshape((2, row_size) + tiles.shape[1:]).swapaxes(0, 1)
    tiles = jnp.concatenate((tiles, tiles), axis=0)
    outgoing = lax.dynamic_slice_in_dim(tiles, row_size - place, row_size, 0)
    incoming = lax.all_to_all(outgoing, row_axis, 0, 0).astype(jnp.float32)
    same = (chunk_ids <= place)[:, None, None, None, None]
    first = incoming[:, 0]
    second = incoming[:, 1]
    own_rows = jnp.sum(jnp.where(same, first, 0.0), axis=0)
    spills = [
        jnp.sum(jnp.where(same, second, first), axis=0),
        jnp.sum(jnp.where(same, 0.0, second), axis=0),
    ]
    for ahead, spill in zip((1, 2), spills):
        own_rows = own_rows + lax.ppermute(
            spill.astype(jnp.bfloat16),
            tile_axes,
            [(s, (s + ahead * row_size) % tile_count) for s in range(tile_count)],
        ).astype(jnp.float32)
    return jnp.transpose(own_rows, (1, 0, 2, 3))


def row_length(devices):
    places = sorted({device.coords[0] for device in devices})
    return len(places)


def solution(mesh):
    sections, tiles = mesh.devices.shape
    row_size = row_length(list(mesh.devices[0]))
    grid = mesh.devices.reshape(sections, tiles // row_size, row_size)
    grid_mesh = jax.sharding.Mesh(grid, ("section", "lines", "x"))
    tile_axes = ("lines", "x")
    return jax.shard_map(
        functools.partial(on_device, "x", tile_axes),
        mesh=grid_mesh,
        in_specs=(
            P(),
            P(),
            P("section", tile_axes, None, None),
            P(tile_axes),
            P(tile_axes),
            P(tile_axes, None, None),
        ),
        out_specs=P("section", tile_axes, None, None),
        check_vma=False,
    )
```

```python
import functools

import jax
from jax.experimental import pallas as pl
import jax.numpy as jnp
from jax import lax
from jax.sharding import PartitionSpec as P


def shifted(value, axis, steps):
    count = lax.axis_size(axis)
    pairs = [(source, (source + steps) % count) for source in range(count)]
    return lax.ppermute(value, axis, pairs)


def passed_along(shard, axis, by):
    length = lax.axis_size(axis)
    pairs = [(i, i + by) for i in range(length) if 0 <= i + by < length]
    return lax.ppermute(shard, axis, pairs)


def dft_matrix(length):
    points = jnp.arange(length, dtype=jnp.int32)
    product_mod = points[:, None] * points[None, :] % length
    angle = 2.0 * 3.141592653589793 / length * product_mod.astype(jnp.float32)
    scale_fac = 1.0 / jnp.sqrt(jnp.float32(length))
    return jnp.stack((jnp.cos(angle) * scale_fac, -jnp.sin(angle) * scale_fac)).astype(jnp.bfloat16)


def product(form, first, second):
    return jnp.einsum(form, first, second, preferred_element_type=jnp.float32)


def apply_left(matrix, field):
    first_part = product("ij,...jck->...ick", matrix[0], field)
    second_part = product("ij,...jck->...ick", matrix[1], field)
    return jnp.stack(
        (
            first_part[..., 0, :] - second_part[..., 1, :],
            first_part[..., 1, :] + second_part[..., 0, :],
        ),
        axis=-2,
    )


def apply_left_adj(matrix, field):
    first_part = product("ji,...jck->...ick", matrix[0], field)
    second_part = product("ji,...jck->...ick", matrix[1], field)
    return jnp.stack(
        (
            first_part[..., 0, :] + second_part[..., 1, :],
            first_part[..., 1, :] - second_part[..., 0, :],
        ),
        axis=-2,
    )


def apply_right(field, matrix):
    first_part = product("...ick,lk->...icl", field, matrix[0])
    second_part = product("...ick,lk->...icl", field, matrix[1])
    return jnp.stack(
        (
            first_part[..., 0, :] - second_part[..., 1, :],
            second_part[..., 0, :] + first_part[..., 1, :],
        ),
        axis=-2,
    )


def apply_right_conj(field, matrix):
    first_part = product("...ick,kl->...icl", field, matrix[0])
    second_part = product("...ick,kl->...icl", field, matrix[1])
    return jnp.stack(
        (
            first_part[..., 0, :] + second_part[..., 1, :],
            first_part[..., 1, :] - second_part[..., 0, :],
        ),
        axis=-2,
    )


def complex_mul(first, second):
    first = first.astype(jnp.float32)
    second = second.astype(jnp.float32)
    return jnp.stack(
        (
            first[..., 0, :] * second[..., 0, :] - first[..., 1, :] * second[..., 1, :],
            first[..., 0, :] * second[..., 1, :] + first[..., 1, :] * second[..., 0, :],
        ),
        axis=-2,
    )


def conj_mul(first, second):
    first = first.astype(jnp.float32)
    return jnp.stack(
        (
            first[..., 0, :] * second[..., 0, :] + first[..., 1, :] * second[..., 1, :],
            first[..., 0, :] * second[..., 1, :] - first[..., 1, :] * second[..., 0, :],
        ),
        axis=-2,
    )


def accumulate(gradients, starts, buffer_rows):
    width = gradients.shape[-1]
    margin = buffer_rows - width
    placed = jnp.transpose(gradients[0], (1, 0, 2, 3))
    padded = jnp.pad(placed, ((margin, margin), (0, 0), (0, 0), (0, 0)))
    return lax.dynamic_slice_in_dim(padded, margin - starts[0], buffer_rows, 0)


def real_dot(first, second):
    return jnp.dot(first, second, preferred_element_type=jnp.float32)


def times_left(stacked, field_real, field_imag):
    side = field_real.shape[0]
    with_real = real_dot(stacked, field_real)
    with_imag = real_dot(stacked, field_imag)
    return (
        with_real[:side] - with_imag[side:],
        with_imag[:side] + with_real[side:],
    )


def times_left_adj(stacked_t, field_real, field_imag):
    side = field_real.shape[0]
    with_real = real_dot(stacked_t, field_real)
    with_imag = real_dot(stacked_t, field_imag)
    return (
        with_real[:side] + with_imag[side:],
        with_imag[:side] - with_real[side:],
    )


def times_right(field_real, field_imag, real_t, imag_t):
    side = field_real.shape[0]
    both = jnp.concatenate((field_real, field_imag), axis=0)
    with_real = real_dot(both, real_t)
    with_imag = real_dot(both, imag_t)
    return (
        with_real[:side] - with_imag[side:],
        with_imag[:side] + with_real[side:],
    )


def times_right_conj(field_real, field_imag, real, imag):
    side = field_real.shape[0]
    both = jnp.concatenate((field_real, field_imag), axis=0)
    with_real = real_dot(both, real)
    with_imag = real_dot(both, imag)
    return (
        with_real[:side] + with_imag[side:],
        with_real[side:] - with_imag[:side],
    )


def rounded(pair):
    return (pair[0].astype(jnp.bfloat16), pair[1].astype(jnp.bfloat16))


def march_steps(field, patch_ref, mats, incident_ref):
    stacked, stacked_t, real, imag, real_t, imag_t = mats
    field_real, field_imag = field
    for slice_at in range(patch_ref.shape[0]):
        incident_ref[slice_at, 0] = field_real
        incident_ref[slice_at, 1] = field_imag
        first_real = field_real.astype(jnp.float32)
        first_imag = field_imag.astype(jnp.float32)
        second_real = patch_ref[slice_at, 0].astype(jnp.float32)
        second_imag = patch_ref[slice_at, 1].astype(jnp.float32)
        phase = rounded(
            (
                first_real * second_real - first_imag * second_imag,
                first_real * second_imag + first_imag * second_real,
            )
        )
        middle = rounded(times_left(stacked, *phase))
        field_real, field_imag = rounded(times_right(*middle, real_t, imag_t))
    return (field_real, field_imag)


def far_steps(field, measured, mats):
    stacked, stacked_t, real, imag, real_t, imag_t = mats
    half_far = rounded(times_left(stacked, *field))
    far_real, far_imag = times_right(*half_far, real_t, imag_t)
    misfit = far_real * far_real + far_imag * far_imag - measured.astype(jnp.float32)
    grad_far = rounded((far_real * misfit, far_imag * misfit))
    half_back = rounded(times_left_adj(stacked_t, *grad_far))
    return rounded(times_right_conj(*half_back, real, imag))


def retreat_steps(back, patch_ref, incident_ref, mats, grad_ref):
    stacked, stacked_t, real, imag, real_t, imag_t = mats
    for slice_at in reversed(range(patch_ref.shape[0])):
        middle = rounded(times_left_adj(stacked_t, *back))
        bar_real, bar_imag = times_right_conj(*middle, real, imag)
        inc_real = incident_ref[slice_at, 0].astype(jnp.float32)
        inc_imag = incident_ref[slice_at, 1].astype(jnp.float32)
        grad_ref[slice_at, 0] = inc_real * bar_real + inc_imag * bar_imag
        grad_ref[slice_at, 1] = inc_real * bar_imag - inc_imag * bar_real
        pat_real = patch_ref[slice_at, 0].astype(jnp.float32)
        pat_imag = patch_ref[slice_at, 1].astype(jnp.float32)
        back = rounded(
            (pat_real * bar_real + pat_imag * bar_imag, pat_real * bar_imag - pat_imag * bar_real)
        )
    return back


def mats_of(mat_ref):
    stacked, stacked_t = mat_ref[0], mat_ref[1]
    side = stacked.shape[1]
    return (stacked, stacked_t, stacked[:side], stacked[side:], stacked_t[:side], stacked_t[side:])


def march_kernel(field_ref, patch_ref, mat_ref, out_ref, incident_ref):
    field = march_steps((field_ref[0], field_ref[1]), patch_ref, mats_of(mat_ref), incident_ref)
    out_ref[0] = field[0]
    out_ref[1] = field[1]


def middle_kernel(
    field_ref, patch_ref, mat_ref, measured_ref, dft_ref, out_ref, grad_ref, incident_ref
):
    mats = mats_of(mat_ref)
    field = march_steps((field_ref[0], field_ref[1]), patch_ref, mats, incident_ref)
    back = far_steps(field, measured_ref[...], mats_of(dft_ref))
    back = retreat_steps(back, patch_ref, incident_ref, mats, grad_ref)
    out_ref[0] = back[0]
    out_ref[1] = back[1]


def retreat_kernel(back_ref, patch_ref, incident_ref, mat_ref, out_ref, grad_ref):
    back = retreat_steps(
        (back_ref[0], back_ref[1]), patch_ref, incident_ref, mats_of(mat_ref), grad_ref
    )
    out_ref[0] = back[0]
    out_ref[1] = back[1]


def planes_of(matrix):
    stacked = jnp.concatenate((matrix[0], matrix[1]), axis=0)
    stacked_t = jnp.concatenate((matrix[0].T, matrix[1].T), axis=0)
    return jnp.stack((stacked, stacked_t))


def run_kernel(body, outs, flops, *args):
    moved = sum(arg.size * arg.dtype.itemsize for arg in args)
    listed = outs if isinstance(outs, tuple) else (outs,)
    moved += sum(out.size * jnp.dtype(out.dtype).itemsize for out in listed)
    return pl.pallas_call(
        body,
        out_shape=outs,
        cost_estimate=pl.CostEstimate(flops=flops, transcendentals=0, bytes_accessed=moved),
    )(*args)


def on_device(row_axis, tile_axes, probe, kernel, object_slab, offsets, counts, intensity):
    width = probe.shape[0]
    slot_count = offsets.shape[0]
    local_rows = object_slab.shape[1]
    slice_count = object_slab.shape[0]
    sections = lax.axis_size("section")
    section_now = lax.axis_index("section")
    row_size = lax.axis_size(row_axis)
    tile_count = lax.axis_size(tile_axes)
    tile_now = lax.axis_index(tile_axes)
    place = lax.axis_index(row_axis)
    is_last = section_now == sections - 1
    dft_table = dft_matrix(width)
    chunk_ids = jnp.arange(row_size, dtype=jnp.int32)
    later = [object_slab] + [
        lax.ppermute(
            object_slab,
            tile_axes,
            [(s, (s - ahead * row_size) % tile_count) for s in range(tile_count)],
        )
        for ahead in (1, 2)
    ]
    own_row = (chunk_ids <= place)[:, None, None, None, None, None]
    sent = jnp.where(
        own_row, jnp.stack(later[:2])[None], jnp.stack(later[1:])[None]
    )
    got = lax.all_to_all(sent, row_axis, 0, 0)
    got = lax.dynamic_slice_in_dim(jnp.concatenate((got, got), axis=0), place, row_size, 0)
    window = jnp.concatenate(
        [got[at % row_size, at // row_size] for at in range(2 * row_size)], axis=1
    )
    relative = offsets - tile_now * local_rows
    patches = jax.vmap(lambda offset: lax.dynamic_slice_in_dim(window, offset, width, 1))(relative)
    live_slots = jnp.arange(slot_count, dtype=jnp.int32) < counts[0]

    planes = jnp.transpose(patches[0], (0, 2, 1, 3))
    kernel_planes = planes_of(kernel)
    dft_planes = planes_of(dft_matrix(width))
    field_shape = jax.ShapeDtypeStruct((2, width, width), jnp.bfloat16)
    dot_flops = 2 * width**3

    def march(field_in):
        outs = (field_shape, jax.ShapeDtypeStruct(planes.shape, jnp.bfloat16))
        flops = slice_count * 8 * dot_flops
        return tuple(run_kernel(march_kernel, outs, flops, field_in, planes, kernel_planes))

    def retreat(back_in, incidents):
        outs = (field_shape, jax.ShapeDtypeStruct(planes.shape, jnp.float32))
        flops = slice_count * 8 * dot_flops
        return tuple(
            run_kernel(retreat_kernel, outs, flops, back_in, planes, incidents, kernel_planes)
        )

    def whole(field_in):
        outs = (
            field_shape,
            jax.ShapeDtypeStruct(planes.shape, jnp.float32),
            jax.ShapeDtypeStruct(planes.shape, jnp.bfloat16),
        )
        flops = slice_count * 16 * dot_flops + 16 * dot_flops
        back, grads, _ = run_kernel(
            middle_kernel, outs, flops, field_in, planes, kernel_planes, intensity[0], dft_planes
        )
        return (back, grads)

    stored = jnp.zeros(planes.shape, jnp.bfloat16)
    gradients = jnp.zeros(planes.shape, jnp.float32)
    waves = jnp.transpose(probe, (1, 0, 2))
    for section_step in range(sections - 1):
        if section_step > 0:
            waves = passed_along(waves, "section", 1)
        waves, stored = lax.cond(
            section_now == section_step,
            lambda field_in, kept: march(field_in),
            lambda field_in, kept: (field_in, kept),
            waves,
            stored,
        )
    waves = passed_along(waves, "section", 1)
    adjoints, gradients = lax.cond(
        is_last,
        lambda field_in, kept: whole(field_in),
        lambda field_in, kept: (field_in, kept),
        waves,
        gradients,
    )
    for section_step in reversed(range(sections - 1)):
        adjoints = passed_along(adjoints, "section", -1)
        adjoints, gradients = lax.cond(
            section_now == section_step,
            lambda field_in, kept: retreat(field_in, stored),
            lambda field_in, kept: (field_in, kept),
            adjoints,
            gradients,
        )
    gradients = jnp.transpose(gradients, (0, 2, 1, 3))[None]
    gradients = gradients * live_slots.astype(jnp.float32)[:, None, None, None, None]
    nearby = accumulate(gradients, offsets - tile_now * local_rows, 2 * row_size * local_rows)
    tiles = jnp.stack(
        [nearby[at * local_rows : (at + 1) * local_rows] for at in range(2 * row_size)], axis=0
    ).astype(jnp.bfloat16)
    tiles = tiles.reshape((2, row_size) + tiles.shape[1:]).swapaxes(0, 1)
    tiles = jnp.concatenate((tiles, tiles), axis=0)
    outgoing = lax.dynamic_slice_in_dim(tiles, row_size - place, row_size, 0)
    incoming = lax.all_to_all(outgoing, row_axis, 0, 0).astype(jnp.float32)
    same = (chunk_ids <= place)[:, None, None, None, None]
    first = incoming[:, 0]
    second = incoming[:, 1]
    own_rows = jnp.sum(jnp.where(same, first, 0.0), axis=0)
    spills = [
        jnp.sum(jnp.where(same, second, first), axis=0),
        jnp.sum(jnp.where(same, 0.0, second), axis=0),
    ]
    for ahead, spill in zip((1, 2), spills):
        own_rows = own_rows + lax.ppermute(
            spill.astype(jnp.bfloat16),
            tile_axes,
            [(s, (s + ahead * row_size) % tile_count) for s in range(tile_count)],
        ).astype(jnp.float32)
    return jnp.transpose(own_rows, (1, 0, 2, 3))


def row_length(devices):
    places = sorted({device.coords[0] for device in devices})
    return len(places)


def solution(mesh):
    sections, tiles = mesh.devices.shape
    row_size = row_length(list(mesh.devices[0]))
    grid = mesh.devices.reshape(sections, tiles // row_size, row_size)
    grid_mesh = jax.sharding.Mesh(grid, ("section", "lines", "x"))
    tile_axes = ("lines", "x")
    return jax.shard_map(
        functools.partial(on_device, "x", tile_axes),
        mesh=grid_mesh,
        in_specs=(
            P(),
            P(),
            P("section", tile_axes, None, None),
            P(tile_axes),
            P(tile_axes),
            P(tile_axes, None, None),
        ),
        out_specs=P("section", tile_axes, None, None),
        check_vma=False,
    )
```

```python
import functools

import jax
from jax.experimental import pallas as pl
import jax.numpy as jnp
from jax import lax
from jax.sharding import PartitionSpec as P


def shifted(value, axis, steps):
    count = lax.axis_size(axis)
    pairs = [(source, (source + steps) % count) for source in range(count)]
    return lax.ppermute(value, axis, pairs)


def passed_along(shard, axis, by):
    length = lax.axis_size(axis)
    pairs = [(i, i + by) for i in range(length) if 0 <= i + by < length]
    return lax.ppermute(shard, axis, pairs)


def dft_matrix(length):
    points = jnp.arange(length, dtype=jnp.int32)
    product_mod = points[:, None] * points[None, :] % length
    angle = 2.0 * 3.141592653589793 / length * product_mod.astype(jnp.float32)
    scale_fac = 1.0 / jnp.sqrt(jnp.float32(length))
    return jnp.stack((jnp.cos(angle) * scale_fac, -jnp.sin(angle) * scale_fac)).astype(jnp.bfloat16)


def product(form, first, second):
    return jnp.einsum(form, first, second, preferred_element_type=jnp.float32)


def apply_left(matrix, field):
    first_part = product("ij,...jck->...ick", matrix[0], field)
    second_part = product("ij,...jck->...ick", matrix[1], field)
    return jnp.stack(
        (
            first_part[..., 0, :] - second_part[..., 1, :],
            first_part[..., 1, :] + second_part[..., 0, :],
        ),
        axis=-2,
    )


def apply_left_adj(matrix, field):
    first_part = product("ji,...jck->...ick", matrix[0], field)
    second_part = product("ji,...jck->...ick", matrix[1], field)
    return jnp.stack(
        (
            first_part[..., 0, :] + second_part[..., 1, :],
            first_part[..., 1, :] - second_part[..., 0, :],
        ),
        axis=-2,
    )


def apply_right(field, matrix):
    first_part = product("...ick,lk->...icl", field, matrix[0])
    second_part = product("...ick,lk->...icl", field, matrix[1])
    return jnp.stack(
        (
            first_part[..., 0, :] - second_part[..., 1, :],
            second_part[..., 0, :] + first_part[..., 1, :],
        ),
        axis=-2,
    )


def apply_right_conj(field, matrix):
    first_part = product("...ick,kl->...icl", field, matrix[0])
    second_part = product("...ick,kl->...icl", field, matrix[1])
    return jnp.stack(
        (
            first_part[..., 0, :] + second_part[..., 1, :],
            first_part[..., 1, :] - second_part[..., 0, :],
        ),
        axis=-2,
    )


def complex_mul(first, second):
    first = first.astype(jnp.float32)
    second = second.astype(jnp.float32)
    return jnp.stack(
        (
            first[..., 0, :] * second[..., 0, :] - first[..., 1, :] * second[..., 1, :],
            first[..., 0, :] * second[..., 1, :] + first[..., 1, :] * second[..., 0, :],
        ),
        axis=-2,
    )


def conj_mul(first, second):
    first = first.astype(jnp.float32)
    return jnp.stack(
        (
            first[..., 0, :] * second[..., 0, :] + first[..., 1, :] * second[..., 1, :],
            first[..., 0, :] * second[..., 1, :] - first[..., 1, :] * second[..., 0, :],
        ),
        axis=-2,
    )


def accumulate(gradients, starts, buffer_rows):
    width = gradients.shape[-1]
    margin = buffer_rows - width
    placed = jnp.transpose(gradients[0], (1, 0, 2, 3))
    padded = jnp.pad(placed, ((margin, margin), (0, 0), (0, 0), (0, 0)))
    return lax.dynamic_slice_in_dim(padded, margin - starts[0], buffer_rows, 0)


def real_dot(first, second):
    return jnp.dot(first, second, preferred_element_type=jnp.float32)


def times_left(real, imag, field_real, field_imag):
    return (
        real_dot(real, field_real) - real_dot(imag, field_imag),
        real_dot(real, field_imag) + real_dot(imag, field_real),
    )


def times_left_adj(real_t, imag_t, field_real, field_imag):
    return (
        real_dot(real_t, field_real) + real_dot(imag_t, field_imag),
        real_dot(real_t, field_imag) - real_dot(imag_t, field_real),
    )


def times_right(field_real, field_imag, real_t, imag_t):
    return (
        real_dot(field_real, real_t) - real_dot(field_imag, imag_t),
        real_dot(field_real, imag_t) + real_dot(field_imag, real_t),
    )


def times_right_conj(field_real, field_imag, real, imag):
    return (
        real_dot(field_real, real) + real_dot(field_imag, imag),
        real_dot(field_imag, real) - real_dot(field_real, imag),
    )


def rounded(pair):
    return (pair[0].astype(jnp.bfloat16), pair[1].astype(jnp.bfloat16))


def march_steps(field, patch_ref, mats, incident_ref):
    real, imag, real_t, imag_t = mats
    field_real, field_imag = field
    for slice_at in range(patch_ref.shape[0]):
        incident_ref[slice_at, 0] = field_real
        incident_ref[slice_at, 1] = field_imag
        first_real = field_real.astype(jnp.float32)
        first_imag = field_imag.astype(jnp.float32)
        second_real = patch_ref[slice_at, 0].astype(jnp.float32)
        second_imag = patch_ref[slice_at, 1].astype(jnp.float32)
        phase = rounded(
            (
                first_real * second_real - first_imag * second_imag,
                first_real * second_imag + first_imag * second_real,
            )
        )
        middle = rounded(times_left(real, imag, *phase))
        field_real, field_imag = rounded(times_right(*middle, real_t, imag_t))
    return (field_real, field_imag)


def far_steps(field, measured, mats):
    real, imag, real_t, imag_t = mats
    half_far = rounded(times_left(real, imag, *field))
    far_real, far_imag = times_right(*half_far, real_t, imag_t)
    misfit = far_real * far_real + far_imag * far_imag - measured.astype(jnp.float32)
    grad_far = rounded((far_real * misfit, far_imag * misfit))
    half_back = rounded(times_left_adj(real_t, imag_t, *grad_far))
    return rounded(times_right_conj(*half_back, real, imag))


def retreat_steps(back, patch_ref, incident_ref, mats, grad_ref):
    real, imag, real_t, imag_t = mats
    for slice_at in reversed(range(patch_ref.shape[0])):
        middle = rounded(times_left_adj(real_t, imag_t, *back))
        bar_real, bar_imag = times_right_conj(*middle, real, imag)
        inc_real = incident_ref[slice_at, 0].astype(jnp.float32)
        inc_imag = incident_ref[slice_at, 1].astype(jnp.float32)
        grad_ref[slice_at, 0] = inc_real * bar_real + inc_imag * bar_imag
        grad_ref[slice_at, 1] = inc_real * bar_imag - inc_imag * bar_real
        pat_real = patch_ref[slice_at, 0].astype(jnp.float32)
        pat_imag = patch_ref[slice_at, 1].astype(jnp.float32)
        back = rounded(
            (pat_real * bar_real + pat_imag * bar_imag, pat_real * bar_imag - pat_imag * bar_real)
        )
    return back


def mats_of(mat_ref):
    return (mat_ref[0], mat_ref[1], mat_ref[2], mat_ref[3])


def march_kernel(field_ref, patch_ref, mat_ref, out_ref, incident_ref):
    field = march_steps((field_ref[0], field_ref[1]), patch_ref, mats_of(mat_ref), incident_ref)
    out_ref[0] = field[0]
    out_ref[1] = field[1]


def middle_kernel(
    field_ref, patch_ref, mat_ref, measured_ref, dft_ref, out_ref, grad_ref, incident_ref
):
    mats = mats_of(mat_ref)
    field = march_steps((field_ref[0], field_ref[1]), patch_ref, mats, incident_ref)
    back = far_steps(field, measured_ref[...], mats_of(dft_ref))
    back = retreat_steps(back, patch_ref, incident_ref, mats, grad_ref)
    out_ref[0] = back[0]
    out_ref[1] = back[1]


def retreat_kernel(back_ref, patch_ref, incident_ref, mat_ref, out_ref, grad_ref):
    back = retreat_steps(
        (back_ref[0], back_ref[1]), patch_ref, incident_ref, mats_of(mat_ref), grad_ref
    )
    out_ref[0] = back[0]
    out_ref[1] = back[1]


def planes_of(matrix):
    return jnp.stack((matrix[0], matrix[1], matrix[0].T, matrix[1].T))


def run_kernel(body, outs, flops, *args):
    moved = sum(arg.size * arg.dtype.itemsize for arg in args)
    listed = outs if isinstance(outs, tuple) else (outs,)
    moved += sum(out.size * jnp.dtype(out.dtype).itemsize for out in listed)
    return pl.pallas_call(
        body,
        out_shape=outs,
        cost_estimate=pl.CostEstimate(flops=flops, transcendentals=0, bytes_accessed=moved),
    )(*args)


def on_device(row_axis, tile_axes, probe, kernel, object_slab, offsets, counts, intensity):
    width = probe.shape[0]
    slot_count = offsets.shape[0]
    local_rows = object_slab.shape[1]
    slice_count = object_slab.shape[0]
    sections = lax.axis_size("section")
    section_now = lax.axis_index("section")
    row_size = lax.axis_size(row_axis)
    tile_count = lax.axis_size(tile_axes)
    tile_now = lax.axis_index(tile_axes)
    place = lax.axis_index(row_axis)
    is_last = section_now == sections - 1
    dft_table = dft_matrix(width)
    chunk_ids = jnp.arange(row_size, dtype=jnp.int32)
    slab = jnp.transpose(object_slab, (0, 2, 1, 3))
    later = [slab] + [
        lax.ppermute(
            slab,
            tile_axes,
            [(s, (s - ahead * row_size) % tile_count) for s in range(tile_count)],
        )
        for ahead in (1, 2)
    ]
    own_row = (chunk_ids <= place)[:, None, None, None, None, None]
    sent = jnp.where(own_row, jnp.stack(later[:2])[None], jnp.stack(later[1:])[None])
    got = lax.all_to_all(sent, row_axis, 0, 0)
    got = lax.dynamic_slice_in_dim(jnp.concatenate((got, got), axis=0), place, row_size, 0)
    window = jnp.concatenate(
        [got[at % row_size, at // row_size] for at in range(2 * row_size)], axis=2
    )
    relative = offsets - tile_now * local_rows
    planes = lax.dynamic_slice_in_dim(window, relative[0], width, 2)
    live_slots = jnp.arange(slot_count, dtype=jnp.int32) < counts[0]

    kernel_planes = planes_of(kernel)
    dft_planes = planes_of(dft_matrix(width))
    field_shape = jax.ShapeDtypeStruct((2, width, width), jnp.bfloat16)
    dot_flops = 2 * width**3

    def march(field_in):
        outs = (field_shape, jax.ShapeDtypeStruct(planes.shape, jnp.bfloat16))
        flops = slice_count * 8 * dot_flops
        return tuple(run_kernel(march_kernel, outs, flops, field_in, planes, kernel_planes))

    def retreat(back_in, incidents):
        outs = (field_shape, jax.ShapeDtypeStruct(planes.shape, jnp.float32))
        flops = slice_count * 8 * dot_flops
        return tuple(
            run_kernel(retreat_kernel, outs, flops, back_in, planes, incidents, kernel_planes)
        )

    def whole(field_in):
        outs = (
            field_shape,
            jax.ShapeDtypeStruct(planes.shape, jnp.float32),
            jax.ShapeDtypeStruct(planes.shape, jnp.bfloat16),
        )
        flops = slice_count * 16 * dot_flops + 16 * dot_flops
        back, grads, _ = run_kernel(
            middle_kernel, outs, flops, field_in, planes, kernel_planes, intensity[0], dft_planes
        )
        return (back, grads)

    stored = jnp.zeros(planes.shape, jnp.bfloat16)
    gradients = jnp.zeros(planes.shape, jnp.float32)
    waves = jnp.transpose(probe, (1, 0, 2))
    for section_step in range(sections - 1):
        if section_step > 0:
            waves = passed_along(waves, "section", 1)
        waves, stored = lax.cond(
            section_now == section_step,
            lambda field_in, kept: march(field_in),
            lambda field_in, kept: (field_in, kept),
            waves,
            stored,
        )
    waves = passed_along(waves, "section", 1)
    adjoints, gradients = lax.cond(
        is_last,
        lambda field_in, kept: whole(field_in),
        lambda field_in, kept: (field_in, kept),
        waves,
        gradients,
    )
    for section_step in reversed(range(sections - 1)):
        adjoints = passed_along(adjoints, "section", -1)
        adjoints, gradients = lax.cond(
            section_now == section_step,
            lambda field_in, kept: retreat(field_in, stored),
            lambda field_in, kept: (field_in, kept),
            adjoints,
            gradients,
        )
    gradients = gradients * live_slots[0].astype(jnp.float32)
    span = 2 * row_size * local_rows
    margin = span - width
    padded = jnp.pad(gradients, ((0, 0), (0, 0), (margin, margin), (0, 0)))
    nearby = lax.dynamic_slice_in_dim(padded, margin - relative[0], span, 2)
    tiles = nearby.reshape(nearby.shape[:2] + (2, row_size, local_rows, width))
    tiles = jnp.transpose(tiles, (3, 2, 0, 1, 4, 5)).astype(jnp.bfloat16)
    tiles = jnp.concatenate((tiles, tiles), axis=0)
    outgoing = lax.dynamic_slice_in_dim(tiles, row_size - place, row_size, 0)
    incoming = lax.all_to_all(outgoing, row_axis, 0, 0).astype(jnp.float32)
    same = (chunk_ids <= place)[:, None, None, None, None]
    first = incoming[:, 0]
    second = incoming[:, 1]
    own_rows = jnp.sum(jnp.where(same, first, 0.0), axis=0)
    spills = [
        jnp.sum(jnp.where(same, second, first), axis=0),
        jnp.sum(jnp.where(same, 0.0, second), axis=0),
    ]
    for ahead, spill in zip((1, 2), spills):
        own_rows = own_rows + lax.ppermute(
            spill.astype(jnp.bfloat16),
            tile_axes,
            [(s, (s + ahead * row_size) % tile_count) for s in range(tile_count)],
        ).astype(jnp.float32)
    return jnp.transpose(own_rows, (0, 2, 1, 3))


def row_length(devices):
    places = sorted({device.coords[0] for device in devices})
    return len(places)


def solution(mesh):
    sections, tiles = mesh.devices.shape
    row_size = row_length(list(mesh.devices[0]))
    grid = mesh.devices.reshape(sections, tiles // row_size, row_size)
    grid_mesh = jax.sharding.Mesh(grid, ("section", "lines", "x"))
    tile_axes = ("lines", "x")
    return jax.shard_map(
        functools.partial(on_device, "x", tile_axes),
        mesh=grid_mesh,
        in_specs=(
            P(),
            P(),
            P("section", tile_axes, None, None),
            P(tile_axes),
            P(tile_axes),
            P(tile_axes, None, None),
        ),
        out_specs=P("section", tile_axes, None, None),
        check_vma=False,
    )
```

```python
import functools

import jax
from jax.experimental import pallas as pl
from jax.experimental.pallas import tpu as pltpu
import jax.numpy as jnp
from jax import lax
from jax.sharding import PartitionSpec as P


def shifted(value, axis, steps):
    count = lax.axis_size(axis)
    pairs = [(source, (source + steps) % count) for source in range(count)]
    return lax.ppermute(value, axis, pairs)


def passed_along(shard, axis, by):
    length = lax.axis_size(axis)
    pairs = [(i, i + by) for i in range(length) if 0 <= i + by < length]
    return lax.ppermute(shard, axis, pairs)


def dft_matrix(length):
    points = jnp.arange(length, dtype=jnp.int32)
    product_mod = points[:, None] * points[None, :] % length
    angle = 2.0 * 3.141592653589793 / length * product_mod.astype(jnp.float32)
    scale_fac = 1.0 / jnp.sqrt(jnp.float32(length))
    return jnp.stack((jnp.cos(angle) * scale_fac, -jnp.sin(angle) * scale_fac)).astype(jnp.bfloat16)


def product(form, first, second):
    return jnp.einsum(form, first, second, preferred_element_type=jnp.float32)


def apply_left(matrix, field):
    first_part = product("ij,...jck->...ick", matrix[0], field)
    second_part = product("ij,...jck->...ick", matrix[1], field)
    return jnp.stack(
        (
            first_part[..., 0, :] - second_part[..., 1, :],
            first_part[..., 1, :] + second_part[..., 0, :],
        ),
        axis=-2,
    )


def apply_left_adj(matrix, field):
    first_part = product("ji,...jck->...ick", matrix[0], field)
    second_part = product("ji,...jck->...ick", matrix[1], field)
    return jnp.stack(
        (
            first_part[..., 0, :] + second_part[..., 1, :],
            first_part[..., 1, :] - second_part[..., 0, :],
        ),
        axis=-2,
    )


def apply_right(field, matrix):
    first_part = product("...ick,lk->...icl", field, matrix[0])
    second_part = product("...ick,lk->...icl", field, matrix[1])
    return jnp.stack(
        (
            first_part[..., 0, :] - second_part[..., 1, :],
            second_part[..., 0, :] + first_part[..., 1, :],
        ),
        axis=-2,
    )


def apply_right_conj(field, matrix):
    first_part = product("...ick,kl->...icl", field, matrix[0])
    second_part = product("...ick,kl->...icl", field, matrix[1])
    return jnp.stack(
        (
            first_part[..., 0, :] + second_part[..., 1, :],
            first_part[..., 1, :] - second_part[..., 0, :],
        ),
        axis=-2,
    )


def complex_mul(first, second):
    first = first.astype(jnp.float32)
    second = second.astype(jnp.float32)
    return jnp.stack(
        (
            first[..., 0, :] * second[..., 0, :] - first[..., 1, :] * second[..., 1, :],
            first[..., 0, :] * second[..., 1, :] + first[..., 1, :] * second[..., 0, :],
        ),
        axis=-2,
    )


def conj_mul(first, second):
    first = first.astype(jnp.float32)
    return jnp.stack(
        (
            first[..., 0, :] * second[..., 0, :] + first[..., 1, :] * second[..., 1, :],
            first[..., 0, :] * second[..., 1, :] - first[..., 1, :] * second[..., 0, :],
        ),
        axis=-2,
    )


def accumulate(gradients, starts, buffer_rows):
    width = gradients.shape[-1]
    margin = buffer_rows - width
    placed = jnp.transpose(gradients[0], (1, 0, 2, 3))
    padded = jnp.pad(placed, ((margin, margin), (0, 0), (0, 0), (0, 0)))
    return lax.dynamic_slice_in_dim(padded, margin - starts[0], buffer_rows, 0)


def real_dot(first, second):
    return jnp.dot(first, second, preferred_element_type=jnp.float32)


def times_left(real, imag, field_real, field_imag):
    return (
        real_dot(real, field_real) - real_dot(imag, field_imag),
        real_dot(real, field_imag) + real_dot(imag, field_real),
    )


def times_left_adj(real_t, imag_t, field_real, field_imag):
    return (
        real_dot(real_t, field_real) + real_dot(imag_t, field_imag),
        real_dot(real_t, field_imag) - real_dot(imag_t, field_real),
    )


def times_right(field_real, field_imag, real_t, imag_t):
    return (
        real_dot(field_real, real_t) - real_dot(field_imag, imag_t),
        real_dot(field_real, imag_t) + real_dot(field_imag, real_t),
    )


def times_right_conj(field_real, field_imag, real, imag):
    return (
        real_dot(field_real, real) + real_dot(field_imag, imag),
        real_dot(field_imag, real) - real_dot(field_real, imag),
    )


def rounded(pair):
    return (pair[0].astype(jnp.bfloat16), pair[1].astype(jnp.bfloat16))


def march_steps(field, patch_ref, mats, incident_ref):
    real, imag, real_t, imag_t = mats
    field_real, field_imag = field
    for slice_at in range(patch_ref.shape[0]):
        incident_ref[slice_at, 0] = field_real
        incident_ref[slice_at, 1] = field_imag
        first_real = field_real.astype(jnp.float32)
        first_imag = field_imag.astype(jnp.float32)
        second_real = patch_ref[slice_at, 0].astype(jnp.float32)
        second_imag = patch_ref[slice_at, 1].astype(jnp.float32)
        phase = rounded(
            (
                first_real * second_real - first_imag * second_imag,
                first_real * second_imag + first_imag * second_real,
            )
        )
        middle = rounded(times_left(real, imag, *phase))
        field_real, field_imag = rounded(times_right(*middle, real_t, imag_t))
    return (field_real, field_imag)


def far_steps(field, measured, mats):
    real, imag, real_t, imag_t = mats
    half_far = rounded(times_left(real, imag, *field))
    far_real, far_imag = times_right(*half_far, real_t, imag_t)
    misfit = far_real * far_real + far_imag * far_imag - measured.astype(jnp.float32)
    grad_far = rounded((far_real * misfit, far_imag * misfit))
    half_back = rounded(times_left_adj(real_t, imag_t, *grad_far))
    return rounded(times_right_conj(*half_back, real, imag))


def retreat_steps(back, patch_ref, incident_ref, mats, grad_ref):
    real, imag, real_t, imag_t = mats
    for slice_at in reversed(range(patch_ref.shape[0])):
        middle = rounded(times_left_adj(real_t, imag_t, *back))
        bar_real, bar_imag = times_right_conj(*middle, real, imag)
        inc_real = incident_ref[slice_at, 0].astype(jnp.float32)
        inc_imag = incident_ref[slice_at, 1].astype(jnp.float32)
        grad_ref[slice_at, 0] = (inc_real * bar_real + inc_imag * bar_imag).astype(grad_ref.dtype)
        grad_ref[slice_at, 1] = (inc_real * bar_imag - inc_imag * bar_real).astype(grad_ref.dtype)
        pat_real = patch_ref[slice_at, 0].astype(jnp.float32)
        pat_imag = patch_ref[slice_at, 1].astype(jnp.float32)
        back = rounded(
            (pat_real * bar_real + pat_imag * bar_imag, pat_real * bar_imag - pat_imag * bar_real)
        )
    return back


def mats_of(mat_ref):
    return (mat_ref[0], mat_ref[1], mat_ref[2], mat_ref[3])


def march_kernel(field_ref, patch_ref, mat_ref, out_ref, incident_ref):
    field = march_steps((field_ref[0], field_ref[1]), patch_ref, mats_of(mat_ref), incident_ref)
    out_ref[0] = field[0]
    out_ref[1] = field[1]


def middle_kernel(
    field_ref, patch_ref, mat_ref, measured_ref, dft_ref, out_ref, grad_ref, incident_ref
):
    mats = mats_of(mat_ref)
    field = march_steps((field_ref[0], field_ref[1]), patch_ref, mats, incident_ref)
    dft = (dft_ref[0], dft_ref[1], dft_ref[0], dft_ref[1])
    back = far_steps(field, measured_ref[...], dft)
    back = retreat_steps(back, patch_ref, incident_ref, mats, grad_ref)
    out_ref[0] = back[0]
    out_ref[1] = back[1]


def retreat_kernel(back_ref, patch_ref, incident_ref, mat_ref, out_ref, grad_ref):
    back = retreat_steps(
        (back_ref[0], back_ref[1]), patch_ref, incident_ref, mats_of(mat_ref), grad_ref
    )
    out_ref[0] = back[0]
    out_ref[1] = back[1]


def planes_of(matrix):
    return jnp.stack((matrix[0], matrix[1], matrix[0].T, matrix[1].T))


def run_kernel(body, outs, flops, *args, scratch=()):
    moved = sum(arg.size * arg.dtype.itemsize for arg in args)
    listed = outs if isinstance(outs, tuple) else (outs,)
    moved += sum(out.size * jnp.dtype(out.dtype).itemsize for out in listed)
    return pl.pallas_call(
        body,
        out_shape=outs,
        scratch_shapes=list(scratch),
        cost_estimate=pl.CostEstimate(flops=flops, transcendentals=0, bytes_accessed=moved),
    )(*args)


def on_device(row_axis, tile_axes, probe, kernel, object_slab, offsets, counts, intensity):
    width = probe.shape[0]
    slot_count = offsets.shape[0]
    local_rows = object_slab.shape[1]
    slice_count = object_slab.shape[0]
    sections = lax.axis_size("section")
    section_now = lax.axis_index("section")
    row_size = lax.axis_size(row_axis)
    tile_count = lax.axis_size(tile_axes)
    tile_now = lax.axis_index(tile_axes)
    place = lax.axis_index(row_axis)
    is_last = section_now == sections - 1
    dft_table = dft_matrix(width)
    chunk_ids = jnp.arange(row_size, dtype=jnp.int32)
    slab = jnp.transpose(object_slab, (0, 2, 1, 3))
    later = [slab] + [
        lax.ppermute(
            slab,
            tile_axes,
            [(s, (s - ahead * row_size) % tile_count) for s in range(tile_count)],
        )
        for ahead in (1, 2)
    ]
    own_row = (chunk_ids <= place)[:, None, None, None, None, None]
    sent = jnp.where(own_row, jnp.stack(later[:2])[None], jnp.stack(later[1:])[None])
    got = lax.all_to_all(sent, row_axis, 0, 0)
    got = lax.dynamic_slice_in_dim(jnp.concatenate((got, got), axis=0), place, row_size, 0)
    window = jnp.concatenate(
        [got[at % row_size, at // row_size] for at in range(2 * row_size)], axis=2
    )
    relative = offsets - tile_now * local_rows
    planes = lax.dynamic_slice_in_dim(window, relative[0], width, 2)
    live_slots = jnp.arange(slot_count, dtype=jnp.int32) < counts[0]

    kernel_planes = planes_of(kernel)
    dft_table = dft_matrix(width)
    field_shape = jax.ShapeDtypeStruct((2, width, width), jnp.bfloat16)
    dot_flops = 2 * width**3

    def march(field_in):
        outs = (field_shape, jax.ShapeDtypeStruct(planes.shape, jnp.bfloat16))
        flops = slice_count * 8 * dot_flops
        return tuple(run_kernel(march_kernel, outs, flops, field_in, planes, kernel_planes))

    def retreat(back_in, incidents):
        outs = (field_shape, jax.ShapeDtypeStruct(planes.shape, jnp.bfloat16))
        flops = slice_count * 8 * dot_flops
        return tuple(
            run_kernel(retreat_kernel, outs, flops, back_in, planes, incidents, kernel_planes)
        )

    def whole(field_in):
        outs = (field_shape, jax.ShapeDtypeStruct(planes.shape, jnp.bfloat16))
        flops = slice_count * 16 * dot_flops + 16 * dot_flops
        scratch = (pltpu.VMEM(planes.shape, jnp.bfloat16),)
        back, grads = run_kernel(
            middle_kernel,
            outs,
            flops,
            field_in,
            planes,
            kernel_planes,
            intensity[0],
            dft_table,
            scratch=scratch,
        )
        return (back, grads)

    stored = jnp.zeros(planes.shape, jnp.bfloat16)
    gradients = jnp.zeros(planes.shape, jnp.bfloat16)
    waves = jnp.transpose(probe, (1, 0, 2))
    for section_step in range(sections - 1):
        if section_step > 0:
            waves = passed_along(waves, "section", 1)
        waves, stored = lax.cond(
            section_now == section_step,
            lambda field_in, kept: march(field_in),
            lambda field_in, kept: (field_in, kept),
            waves,
            stored,
        )
    waves = passed_along(waves, "section", 1)
    adjoints, gradients = lax.cond(
        is_last,
        lambda field_in, kept: whole(field_in),
        lambda field_in, kept: (field_in, kept),
        waves,
        gradients,
    )
    for section_step in reversed(range(sections - 1)):
        adjoints = passed_along(adjoints, "section", -1)
        adjoints, gradients = lax.cond(
            section_now == section_step,
            lambda field_in, kept: retreat(field_in, stored),
            lambda field_in, kept: (field_in, kept),
            adjoints,
            gradients,
        )
    gradients = gradients * live_slots[0].astype(jnp.float32)
    span = 2 * row_size * local_rows
    margin = span - width
    padded = jnp.pad(gradients, ((0, 0), (0, 0), (margin, margin), (0, 0)))
    nearby = lax.dynamic_slice_in_dim(padded, margin - relative[0], span, 2)
    tiles = nearby.reshape(nearby.shape[:2] + (2, row_size, local_rows, width))
    tiles = jnp.transpose(tiles, (3, 2, 0, 1, 4, 5)).astype(jnp.bfloat16)
    tiles = jnp.concatenate((tiles, tiles), axis=0)
    outgoing = lax.dynamic_slice_in_dim(tiles, row_size - place, row_size, 0)
    incoming = lax.all_to_all(outgoing, row_axis, 0, 0).astype(jnp.float32)
    same = (chunk_ids <= place)[:, None, None, None, None]
    first = incoming[:, 0]
    second = incoming[:, 1]
    own_rows = jnp.sum(jnp.where(same, first, 0.0), axis=0)
    spills = [
        jnp.sum(jnp.where(same, second, first), axis=0),
        jnp.sum(jnp.where(same, 0.0, second), axis=0),
    ]
    for ahead, spill in zip((1, 2), spills):
        own_rows = own_rows + lax.ppermute(
            spill.astype(jnp.bfloat16),
            tile_axes,
            [(s, (s + ahead * row_size) % tile_count) for s in range(tile_count)],
        ).astype(jnp.float32)
    return jnp.transpose(own_rows, (0, 2, 1, 3))


def row_length(devices):
    places = sorted({device.coords[0] for device in devices})
    return len(places)


def solution(mesh):
    sections, tiles = mesh.devices.shape
    row_size = row_length(list(mesh.devices[0]))
    grid = mesh.devices.reshape(sections, tiles // row_size, row_size)
    grid_mesh = jax.sharding.Mesh(grid, ("section", "lines", "x"))
    tile_axes = ("lines", "x")
    return jax.shard_map(
        functools.partial(on_device, "x", tile_axes),
        mesh=grid_mesh,
        in_specs=(
            P(),
            P(),
            P("section", tile_axes, None, None),
            P(tile_axes),
            P(tile_axes),
            P(tile_axes, None, None),
        ),
        out_specs=P("section", tile_axes, None, None),
        check_vma=False,
    )
```

```python
import functools

import jax
from jax.experimental import pallas as pl
from jax.experimental.pallas import tpu as pltpu
import jax.numpy as jnp
from jax import lax
from jax.sharding import PartitionSpec as P


def shifted(value, axis, steps):
    count = lax.axis_size(axis)
    pairs = [(source, (source + steps) % count) for source in range(count)]
    return lax.ppermute(value, axis, pairs)


def passed_along(shard, axis, by):
    length = lax.axis_size(axis)
    pairs = [(i, i + by) for i in range(length) if 0 <= i + by < length]
    return lax.ppermute(shard, axis, pairs)


def dft_matrix(length):
    points = jnp.arange(length, dtype=jnp.int32)
    product_mod = points[:, None] * points[None, :] % length
    angle = 2.0 * 3.141592653589793 / length * product_mod.astype(jnp.float32)
    scale_fac = 1.0 / jnp.sqrt(jnp.float32(length))
    return jnp.stack((jnp.cos(angle) * scale_fac, -jnp.sin(angle) * scale_fac)).astype(jnp.bfloat16)


def product(form, first, second):
    return jnp.einsum(form, first, second, preferred_element_type=jnp.float32)


def apply_left(matrix, field):
    first_part = product("ij,...jck->...ick", matrix[0], field)
    second_part = product("ij,...jck->...ick", matrix[1], field)
    return jnp.stack(
        (
            first_part[..., 0, :] - second_part[..., 1, :],
            first_part[..., 1, :] + second_part[..., 0, :],
        ),
        axis=-2,
    )


def apply_left_adj(matrix, field):
    first_part = product("ji,...jck->...ick", matrix[0], field)
    second_part = product("ji,...jck->...ick", matrix[1], field)
    return jnp.stack(
        (
            first_part[..., 0, :] + second_part[..., 1, :],
            first_part[..., 1, :] - second_part[..., 0, :],
        ),
        axis=-2,
    )


def apply_right(field, matrix):
    first_part = product("...ick,lk->...icl", field, matrix[0])
    second_part = product("...ick,lk->...icl", field, matrix[1])
    return jnp.stack(
        (
            first_part[..., 0, :] - second_part[..., 1, :],
            second_part[..., 0, :] + first_part[..., 1, :],
        ),
        axis=-2,
    )


def apply_right_conj(field, matrix):
    first_part = product("...ick,kl->...icl", field, matrix[0])
    second_part = product("...ick,kl->...icl", field, matrix[1])
    return jnp.stack(
        (
            first_part[..., 0, :] + second_part[..., 1, :],
            first_part[..., 1, :] - second_part[..., 0, :],
        ),
        axis=-2,
    )


def complex_mul(first, second):
    first = first.astype(jnp.float32)
    second = second.astype(jnp.float32)
    return jnp.stack(
        (
            first[..., 0, :] * second[..., 0, :] - first[..., 1, :] * second[..., 1, :],
            first[..., 0, :] * second[..., 1, :] + first[..., 1, :] * second[..., 0, :],
        ),
        axis=-2,
    )


def conj_mul(first, second):
    first = first.astype(jnp.float32)
    return jnp.stack(
        (
            first[..., 0, :] * second[..., 0, :] + first[..., 1, :] * second[..., 1, :],
            first[..., 0, :] * second[..., 1, :] - first[..., 1, :] * second[..., 0, :],
        ),
        axis=-2,
    )


def accumulate(gradients, starts, buffer_rows):
    width = gradients.shape[-1]
    margin = buffer_rows - width
    placed = jnp.transpose(gradients[0], (1, 0, 2, 3))
    padded = jnp.pad(placed, ((margin, margin), (0, 0), (0, 0), (0, 0)))
    return lax.dynamic_slice_in_dim(padded, margin - starts[0], buffer_rows, 0)


def real_dot(first, second):
    return jnp.dot(first, second, preferred_element_type=jnp.float32)


def times_left(real, imag, field_real, field_imag):
    return (
        real_dot(real, field_real) - real_dot(imag, field_imag),
        real_dot(real, field_imag) + real_dot(imag, field_real),
    )


def times_left_adj(real_t, imag_t, field_real, field_imag):
    return (
        real_dot(real_t, field_real) + real_dot(imag_t, field_imag),
        real_dot(real_t, field_imag) - real_dot(imag_t, field_real),
    )


def times_right(field_real, field_imag, real_t, imag_t):
    return (
        real_dot(field_real, real_t) - real_dot(field_imag, imag_t),
        real_dot(field_real, imag_t) + real_dot(field_imag, real_t),
    )


def times_right_conj(field_real, field_imag, real, imag):
    return (
        real_dot(field_real, real) + real_dot(field_imag, imag),
        real_dot(field_imag, real) - real_dot(field_real, imag),
    )


def rounded(pair):
    return (pair[0].astype(jnp.bfloat16), pair[1].astype(jnp.bfloat16))


def march_steps(field, patch_ref, mats, incident_ref):
    real, imag, real_t, imag_t = mats
    field_real, field_imag = field
    for slice_at in range(patch_ref.shape[0]):
        incident_ref[slice_at, 0] = field_real
        incident_ref[slice_at, 1] = field_imag
        first_real = field_real.astype(jnp.float32)
        first_imag = field_imag.astype(jnp.float32)
        second_real = patch_ref[slice_at, 0].astype(jnp.float32)
        second_imag = patch_ref[slice_at, 1].astype(jnp.float32)
        phase = rounded(
            (
                first_real * second_real - first_imag * second_imag,
                first_real * second_imag + first_imag * second_real,
            )
        )
        middle = rounded(times_left(real, imag, *phase))
        field_real, field_imag = rounded(times_right(*middle, real_t, imag_t))
    return (field_real, field_imag)


def far_steps(field, measured, mats):
    real, imag, real_t, imag_t = mats
    half_far = rounded(times_left(real, imag, *field))
    far_real, far_imag = times_right(*half_far, real_t, imag_t)
    misfit = far_real * far_real + far_imag * far_imag - measured.astype(jnp.float32)
    grad_far = rounded((far_real * misfit, far_imag * misfit))
    half_back = rounded(times_left_adj(real_t, imag_t, *grad_far))
    return rounded(times_right_conj(*half_back, real, imag))


def retreat_steps(back, patch_ref, incident_ref, mats, grad_ref):
    real, imag, real_t, imag_t = mats
    for slice_at in reversed(range(patch_ref.shape[0])):
        middle = rounded(times_left_adj(real_t, imag_t, *back))
        bar_real, bar_imag = times_right_conj(*middle, real, imag)
        inc_real = incident_ref[slice_at, 0].astype(jnp.float32)
        inc_imag = incident_ref[slice_at, 1].astype(jnp.float32)
        grad_ref[slice_at, 0] = (inc_real * bar_real + inc_imag * bar_imag).astype(grad_ref.dtype)
        grad_ref[slice_at, 1] = (inc_real * bar_imag - inc_imag * bar_real).astype(grad_ref.dtype)
        pat_real = patch_ref[slice_at, 0].astype(jnp.float32)
        pat_imag = patch_ref[slice_at, 1].astype(jnp.float32)
        back = rounded(
            (pat_real * bar_real + pat_imag * bar_imag, pat_real * bar_imag - pat_imag * bar_real)
        )
    return back


def mats_of(mat_ref):
    return (mat_ref[0], mat_ref[1], mat_ref[2], mat_ref[3])


def march_kernel(field_ref, patch_ref, mat_ref, out_ref, incident_ref):
    field = march_steps((field_ref[0], field_ref[1]), patch_ref, mats_of(mat_ref), incident_ref)
    out_ref[0] = field[0]
    out_ref[1] = field[1]


def middle_kernel(
    field_ref, patch_ref, mat_ref, measured_ref, dft_ref, out_ref, grad_ref, incident_ref
):
    mats = mats_of(mat_ref)
    field = march_steps((field_ref[0], field_ref[1]), patch_ref, mats, incident_ref)
    dft = (dft_ref[0], dft_ref[1], dft_ref[0], dft_ref[1])
    back = far_steps(field, measured_ref[...], dft)
    back = retreat_steps(back, patch_ref, incident_ref, mats, grad_ref)
    out_ref[0] = back[0]
    out_ref[1] = back[1]


def retreat_kernel(back_ref, patch_ref, incident_ref, mat_ref, out_ref, grad_ref):
    back = retreat_steps(
        (back_ref[0], back_ref[1]), patch_ref, incident_ref, mats_of(mat_ref), grad_ref
    )
    out_ref[0] = back[0]
    out_ref[1] = back[1]


def planes_of(matrix):
    return jnp.stack((matrix[0], matrix[1], matrix[0].T, matrix[1].T))


def run_kernel(body, outs, flops, *args, scratch=()):
    moved = sum(arg.size * arg.dtype.itemsize for arg in args)
    listed = outs if isinstance(outs, tuple) else (outs,)
    moved += sum(out.size * jnp.dtype(out.dtype).itemsize for out in listed)
    return pl.pallas_call(
        body,
        out_shape=outs,
        scratch_shapes=list(scratch),
        cost_estimate=pl.CostEstimate(flops=flops, transcendentals=0, bytes_accessed=moved),
    )(*args)


def on_device(row_axis, tile_axes, probe, kernel, object_slab, offsets, counts, intensity):
    width = probe.shape[0]
    slot_count = offsets.shape[0]
    local_rows = object_slab.shape[1]
    slice_count = object_slab.shape[0]
    sections = lax.axis_size("section")
    section_now = lax.axis_index("section")
    row_size = lax.axis_size(row_axis)
    tile_count = lax.axis_size(tile_axes)
    tile_now = lax.axis_index(tile_axes)
    place = lax.axis_index(row_axis)
    is_last = section_now == sections - 1
    dft_table = dft_matrix(width)
    chunk_ids = jnp.arange(row_size, dtype=jnp.int32)
    slab = jnp.transpose(object_slab, (0, 2, 1, 3))
    later = [slab] + [
        lax.ppermute(
            slab,
            tile_axes,
            [(s, (s - ahead * row_size) % tile_count) for s in range(tile_count)],
        )
        for ahead in (1, 2)
    ]
    own_row = (chunk_ids <= place)[:, None, None, None, None]
    sent = jnp.stack(
        [jnp.where(own_row, later[half][None], later[half + 1][None]) for half in (0, 1)], axis=1
    )
    got = lax.all_to_all(sent, row_axis, 0, 0)
    got = lax.dynamic_slice_in_dim(jnp.concatenate((got, got), axis=0), place, row_size, 0)
    window = jnp.concatenate(
        [got[at % row_size, at // row_size] for at in range(2 * row_size)], axis=2
    )
    relative = offsets - tile_now * local_rows
    planes = lax.dynamic_slice_in_dim(window, relative[0], width, 2)
    live_slots = jnp.arange(slot_count, dtype=jnp.int32) < counts[0]

    kernel_planes = planes_of(kernel)
    dft_table = dft_matrix(width)
    field_shape = jax.ShapeDtypeStruct((2, width, width), jnp.bfloat16)
    dot_flops = 2 * width**3

    def march(field_in):
        outs = (field_shape, jax.ShapeDtypeStruct(planes.shape, jnp.bfloat16))
        flops = slice_count * 8 * dot_flops
        return tuple(run_kernel(march_kernel, outs, flops, field_in, planes, kernel_planes))

    def retreat(back_in, incidents):
        outs = (field_shape, jax.ShapeDtypeStruct(planes.shape, jnp.bfloat16))
        flops = slice_count * 8 * dot_flops
        return tuple(
            run_kernel(retreat_kernel, outs, flops, back_in, planes, incidents, kernel_planes)
        )

    def whole(field_in):
        outs = (field_shape, jax.ShapeDtypeStruct(planes.shape, jnp.bfloat16))
        flops = slice_count * 16 * dot_flops + 16 * dot_flops
        scratch = (pltpu.VMEM(planes.shape, jnp.bfloat16),)
        back, grads = run_kernel(
            middle_kernel,
            outs,
            flops,
            field_in,
            planes,
            kernel_planes,
            intensity[0],
            dft_table,
            scratch=scratch,
        )
        return (back, grads)

    stored = jnp.zeros(planes.shape, jnp.bfloat16)
    gradients = jnp.zeros(planes.shape, jnp.bfloat16)
    waves = jnp.transpose(probe, (1, 0, 2))
    for section_step in range(sections - 1):
        if section_step > 0:
            waves = passed_along(waves, "section", 1)
        waves, stored = lax.cond(
            section_now == section_step,
            lambda field_in, kept: march(field_in),
            lambda field_in, kept: (field_in, kept),
            waves,
            stored,
        )
    waves = passed_along(waves, "section", 1)
    adjoints, gradients = lax.cond(
        is_last,
        lambda field_in, kept: whole(field_in),
        lambda field_in, kept: (field_in, kept),
        waves,
        gradients,
    )
    for section_step in reversed(range(sections - 1)):
        adjoints = passed_along(adjoints, "section", -1)
        adjoints, gradients = lax.cond(
            section_now == section_step,
            lambda field_in, kept: retreat(field_in, stored),
            lambda field_in, kept: (field_in, kept),
            adjoints,
            gradients,
        )
    gradients = gradients * live_slots[0].astype(jnp.float32)
    span = 2 * row_size * local_rows
    margin = span - width
    padded = jnp.pad(gradients, ((0, 0), (0, 0), (margin, margin), (0, 0)))
    nearby = lax.dynamic_slice_in_dim(padded, margin - relative[0], span, 2)
    tiles = nearby.reshape(nearby.shape[:2] + (2, row_size, local_rows, width))
    tiles = jnp.transpose(tiles, (3, 2, 0, 1, 4, 5)).astype(jnp.bfloat16)
    tiles = jnp.concatenate((tiles, tiles), axis=0)
    outgoing = lax.dynamic_slice_in_dim(tiles, row_size - place, row_size, 0)
    incoming = lax.all_to_all(outgoing, row_axis, 0, 0).astype(jnp.float32)
    same = (chunk_ids <= place)[:, None, None, None, None]
    first = incoming[:, 0]
    second = incoming[:, 1]
    own_rows = jnp.sum(jnp.where(same, first, 0.0), axis=0)
    spills = [
        jnp.sum(jnp.where(same, second, first), axis=0),
        jnp.sum(jnp.where(same, 0.0, second), axis=0),
    ]
    for ahead, spill in zip((1, 2), spills):
        own_rows = own_rows + lax.ppermute(
            spill.astype(jnp.bfloat16),
            tile_axes,
            [(s, (s + ahead * row_size) % tile_count) for s in range(tile_count)],
        ).astype(jnp.float32)
    return jnp.transpose(own_rows, (0, 2, 1, 3))


def row_length(devices):
    places = sorted({device.coords[0] for device in devices})
    return len(places)


def solution(mesh):
    sections, tiles = mesh.devices.shape
    row_size = row_length(list(mesh.devices[0]))
    grid = mesh.devices.reshape(sections, tiles // row_size, row_size)
    grid_mesh = jax.sharding.Mesh(grid, ("section", "lines", "x"))
    tile_axes = ("lines", "x")
    return jax.shard_map(
        functools.partial(on_device, "x", tile_axes),
        mesh=grid_mesh,
        in_specs=(
            P(),
            P(),
            P("section", tile_axes, None, None),
            P(tile_axes),
            P(tile_axes),
            P(tile_axes, None, None),
        ),
        out_specs=P("section", tile_axes, None, None),
        check_vma=False,
    )
```

```python
import functools

import jax
from jax.experimental import pallas as pl
from jax.experimental.pallas import tpu as pltpu
import jax.numpy as jnp
from jax import lax
from jax.sharding import PartitionSpec as P


def shifted(value, axis, steps):
    count = lax.axis_size(axis)
    pairs = [(source, (source + steps) % count) for source in range(count)]
    return lax.ppermute(value, axis, pairs)


def passed_along(shard, axis, by):
    length = lax.axis_size(axis)
    pairs = [(i, i + by) for i in range(length) if 0 <= i + by < length]
    return lax.ppermute(shard, axis, pairs)


def dft_matrix(length):
    points = jnp.arange(length, dtype=jnp.int32)
    product_mod = points[:, None] * points[None, :] % length
    angle = 2.0 * 3.141592653589793 / length * product_mod.astype(jnp.float32)
    scale_fac = 1.0 / jnp.sqrt(jnp.float32(length))
    return jnp.stack((jnp.cos(angle) * scale_fac, -jnp.sin(angle) * scale_fac)).astype(jnp.bfloat16)


def product(form, first, second):
    return jnp.einsum(form, first, second, preferred_element_type=jnp.float32)


def apply_left(matrix, field):
    first_part = product("ij,...jck->...ick", matrix[0], field)
    second_part = product("ij,...jck->...ick", matrix[1], field)
    return jnp.stack(
        (
            first_part[..., 0, :] - second_part[..., 1, :],
            first_part[..., 1, :] + second_part[..., 0, :],
        ),
        axis=-2,
    )


def apply_left_adj(matrix, field):
    first_part = product("ji,...jck->...ick", matrix[0], field)
    second_part = product("ji,...jck->...ick", matrix[1], field)
    return jnp.stack(
        (
            first_part[..., 0, :] + second_part[..., 1, :],
            first_part[..., 1, :] - second_part[..., 0, :],
        ),
        axis=-2,
    )


def apply_right(field, matrix):
    first_part = product("...ick,lk->...icl", field, matrix[0])
    second_part = product("...ick,lk->...icl", field, matrix[1])
    return jnp.stack(
        (
            first_part[..., 0, :] - second_part[..., 1, :],
            second_part[..., 0, :] + first_part[..., 1, :],
        ),
        axis=-2,
    )


def apply_right_conj(field, matrix):
    first_part = product("...ick,kl->...icl", field, matrix[0])
    second_part = product("...ick,kl->...icl", field, matrix[1])
    return jnp.stack(
        (
            first_part[..., 0, :] + second_part[..., 1, :],
            first_part[..., 1, :] - second_part[..., 0, :],
        ),
        axis=-2,
    )


def complex_mul(first, second):
    first = first.astype(jnp.float32)
    second = second.astype(jnp.float32)
    return jnp.stack(
        (
            first[..., 0, :] * second[..., 0, :] - first[..., 1, :] * second[..., 1, :],
            first[..., 0, :] * second[..., 1, :] + first[..., 1, :] * second[..., 0, :],
        ),
        axis=-2,
    )


def conj_mul(first, second):
    first = first.astype(jnp.float32)
    return jnp.stack(
        (
            first[..., 0, :] * second[..., 0, :] + first[..., 1, :] * second[..., 1, :],
            first[..., 0, :] * second[..., 1, :] - first[..., 1, :] * second[..., 0, :],
        ),
        axis=-2,
    )


def accumulate(gradients, starts, buffer_rows):
    width = gradients.shape[-1]
    margin = buffer_rows - width
    placed = jnp.transpose(gradients[0], (1, 0, 2, 3))
    padded = jnp.pad(placed, ((margin, margin), (0, 0), (0, 0), (0, 0)))
    return lax.dynamic_slice_in_dim(padded, margin - starts[0], buffer_rows, 0)


def real_dot(first, second):
    return jnp.dot(first, second, preferred_element_type=jnp.float32)


def times_left(real, imag, field_real, field_imag):
    return (
        real_dot(real, field_real) - real_dot(imag, field_imag),
        real_dot(real, field_imag) + real_dot(imag, field_real),
    )


def times_left_adj(real_t, imag_t, field_real, field_imag):
    return (
        real_dot(real_t, field_real) + real_dot(imag_t, field_imag),
        real_dot(real_t, field_imag) - real_dot(imag_t, field_real),
    )


def times_right(field_real, field_imag, real_t, imag_t):
    return (
        real_dot(field_real, real_t) - real_dot(field_imag, imag_t),
        real_dot(field_real, imag_t) + real_dot(field_imag, real_t),
    )


def times_right_conj(field_real, field_imag, real, imag):
    return (
        real_dot(field_real, real) + real_dot(field_imag, imag),
        real_dot(field_imag, real) - real_dot(field_real, imag),
    )


def rounded(pair):
    return (pair[0].astype(jnp.bfloat16), pair[1].astype(jnp.bfloat16))


def march_steps(field, patch_ref, mats, incident_ref):
    real, imag, real_t, imag_t = mats
    field_real, field_imag = field
    for slice_at in range(patch_ref.shape[0]):
        incident_ref[slice_at, 0] = field_real
        incident_ref[slice_at, 1] = field_imag
        first_real = field_real.astype(jnp.float32)
        first_imag = field_imag.astype(jnp.float32)
        second_real = patch_ref[slice_at, 0].astype(jnp.float32)
        second_imag = patch_ref[slice_at, 1].astype(jnp.float32)
        phase = rounded(
            (
                first_real * second_real - first_imag * second_imag,
                first_real * second_imag + first_imag * second_real,
            )
        )
        middle = rounded(times_left(real, imag, *phase))
        field_real, field_imag = rounded(times_right(*middle, real_t, imag_t))
    return (field_real, field_imag)


def far_steps(field, measured, mats):
    real, imag, real_t, imag_t = mats
    half_far = rounded(times_left(real, imag, *field))
    far_real, far_imag = times_right(*half_far, real_t, imag_t)
    misfit = far_real * far_real + far_imag * far_imag - measured.astype(jnp.float32)
    grad_far = rounded((far_real * misfit, far_imag * misfit))
    half_back = rounded(times_left_adj(real_t, imag_t, *grad_far))
    return rounded(times_right_conj(*half_back, real, imag))


def retreat_steps(back, patch_ref, incident_ref, mats, grad_ref, keep_back=True):
    real, imag, real_t, imag_t = mats
    for slice_at in reversed(range(patch_ref.shape[0])):
        middle = rounded(times_left_adj(real_t, imag_t, *back))
        bar_real, bar_imag = times_right_conj(*middle, real, imag)
        inc_real = incident_ref[slice_at, 0].astype(jnp.float32)
        inc_imag = incident_ref[slice_at, 1].astype(jnp.float32)
        grad_ref[slice_at, 0] = (inc_real * bar_real + inc_imag * bar_imag).astype(grad_ref.dtype)
        grad_ref[slice_at, 1] = (inc_real * bar_imag - inc_imag * bar_real).astype(grad_ref.dtype)
        if slice_at == 0 and not keep_back:
            break
        pat_real = patch_ref[slice_at, 0].astype(jnp.float32)
        pat_imag = patch_ref[slice_at, 1].astype(jnp.float32)
        back = rounded(
            (pat_real * bar_real + pat_imag * bar_imag, pat_real * bar_imag - pat_imag * bar_real)
        )
    return back


def mats_of(mat_ref):
    return (mat_ref[0], mat_ref[1], mat_ref[2], mat_ref[3])


def march_kernel(field_ref, patch_ref, mat_ref, out_ref, incident_ref):
    field = march_steps((field_ref[0], field_ref[1]), patch_ref, mats_of(mat_ref), incident_ref)
    out_ref[0] = field[0]
    out_ref[1] = field[1]


def middle_kernel(
    field_ref, patch_ref, mat_ref, measured_ref, dft_ref, out_ref, grad_ref, incident_ref
):
    mats = mats_of(mat_ref)
    field = march_steps((field_ref[0], field_ref[1]), patch_ref, mats, incident_ref)
    dft = (dft_ref[0], dft_ref[1], dft_ref[0], dft_ref[1])
    back = far_steps(field, measured_ref[...], dft)
    back = retreat_steps(back, patch_ref, incident_ref, mats, grad_ref)
    out_ref[0] = back[0]
    out_ref[1] = back[1]


def retreat_kernel(back_ref, patch_ref, incident_ref, mat_ref, out_ref, grad_ref):
    back = retreat_steps(
        (back_ref[0], back_ref[1]), patch_ref, incident_ref, mats_of(mat_ref), grad_ref
    )
    out_ref[0] = back[0]
    out_ref[1] = back[1]


def final_retreat_kernel(back_ref, patch_ref, incident_ref, mat_ref, grad_ref):
    retreat_steps(
        (back_ref[0], back_ref[1]), patch_ref, incident_ref, mats_of(mat_ref), grad_ref, False
    )


def planes_of(matrix):
    return jnp.stack((matrix[0], matrix[1], matrix[0].T, matrix[1].T))


def run_kernel(body, outs, flops, *args, scratch=()):
    moved = sum(arg.size * arg.dtype.itemsize for arg in args)
    listed = outs if isinstance(outs, tuple) else (outs,)
    moved += sum(out.size * jnp.dtype(out.dtype).itemsize for out in listed)
    return pl.pallas_call(
        body,
        out_shape=outs,
        scratch_shapes=list(scratch),
        cost_estimate=pl.CostEstimate(flops=flops, transcendentals=0, bytes_accessed=moved),
    )(*args)


def on_device(row_axis, tile_axes, probe, kernel, object_slab, offsets, counts, intensity):
    width = probe.shape[0]
    slot_count = offsets.shape[0]
    local_rows = object_slab.shape[1]
    slice_count = object_slab.shape[0]
    sections = lax.axis_size("section")
    section_now = lax.axis_index("section")
    row_size = lax.axis_size(row_axis)
    tile_count = lax.axis_size(tile_axes)
    tile_now = lax.axis_index(tile_axes)
    place = lax.axis_index(row_axis)
    is_last = section_now == sections - 1
    dft_table = dft_matrix(width)
    chunk_ids = jnp.arange(row_size, dtype=jnp.int32)
    slab = jnp.transpose(object_slab, (0, 2, 1, 3))
    later = [slab] + [
        lax.ppermute(
            slab,
            tile_axes,
            [(s, (s - ahead * row_size) % tile_count) for s in range(tile_count)],
        )
        for ahead in (1, 2)
    ]
    own_row = (chunk_ids <= place)[:, None, None, None, None]
    sent = jnp.stack(
        [jnp.where(own_row, later[half][None], later[half + 1][None]) for half in (0, 1)], axis=1
    )
    got = lax.all_to_all(sent, row_axis, 0, 0)
    got = lax.dynamic_slice_in_dim(jnp.concatenate((got, got), axis=0), place, row_size, 0)
    window = jnp.concatenate(
        [got[at % row_size, at // row_size] for at in range(2 * row_size)], axis=2
    )
    relative = offsets - tile_now * local_rows
    planes = lax.dynamic_slice_in_dim(window, relative[0], width, 2)
    live_slots = jnp.arange(slot_count, dtype=jnp.int32) < counts[0]

    kernel_planes = planes_of(kernel)
    dft_table = dft_matrix(width)
    field_shape = jax.ShapeDtypeStruct((2, width, width), jnp.bfloat16)
    dot_flops = 2 * width**3

    def march(field_in):
        outs = (field_shape, jax.ShapeDtypeStruct(planes.shape, jnp.bfloat16))
        flops = slice_count * 8 * dot_flops
        return tuple(run_kernel(march_kernel, outs, flops, field_in, planes, kernel_planes))

    def retreat(back_in, incidents):
        outs = (field_shape, jax.ShapeDtypeStruct(planes.shape, jnp.bfloat16))
        flops = slice_count * 8 * dot_flops
        return tuple(
            run_kernel(retreat_kernel, outs, flops, back_in, planes, incidents, kernel_planes)
        )

    def whole(field_in):
        outs = (field_shape, jax.ShapeDtypeStruct(planes.shape, jnp.bfloat16))
        flops = slice_count * 16 * dot_flops + 16 * dot_flops
        scratch = (pltpu.VMEM(planes.shape, jnp.bfloat16),)
        back, grads = run_kernel(
            middle_kernel,
            outs,
            flops,
            field_in,
            planes,
            kernel_planes,
            intensity[0],
            dft_table,
            scratch=scratch,
        )
        return (back, grads)

    stored = jnp.zeros(planes.shape, jnp.bfloat16)
    gradients = jnp.zeros(planes.shape, jnp.bfloat16)
    waves = jnp.transpose(probe, (1, 0, 2))
    for section_step in range(sections - 1):
        if section_step > 0:
            waves = passed_along(waves, "section", 1)
        waves, stored = lax.cond(
            section_now == section_step,
            lambda field_in, kept: march(field_in),
            lambda field_in, kept: (field_in, kept),
            waves,
            stored,
        )
    waves = passed_along(waves, "section", 1)
    adjoints, gradients = lax.cond(
        is_last,
        lambda field_in, kept: whole(field_in),
        lambda field_in, kept: (field_in, kept),
        waves,
        gradients,
    )
    def final_retreat(back_in, incidents):
        outs = jax.ShapeDtypeStruct(planes.shape, jnp.bfloat16)
        flops = planes.shape[0] * 8 * dot_flops
        return run_kernel(
            final_retreat_kernel, outs, flops, back_in, planes, incidents, kernel_planes
        )

    for section_step in reversed(range(1, sections - 1)):
        adjoints = passed_along(adjoints, "section", -1)
        adjoints, gradients = lax.cond(
            section_now == section_step,
            lambda field_in, kept: retreat(field_in, stored),
            lambda field_in, kept: (field_in, kept),
            adjoints,
            gradients,
        )
    adjoints = passed_along(adjoints, "section", -1)
    gradients = lax.cond(
        section_now == 0,
        lambda field_in, kept: final_retreat(field_in, stored),
        lambda field_in, kept: kept,
        adjoints,
        gradients,
    )
    gradients = gradients * live_slots[0].astype(jnp.float32)
    span = 2 * row_size * local_rows
    margin = span - width
    padded = jnp.pad(gradients, ((0, 0), (0, 0), (margin, margin), (0, 0)))
    nearby = lax.dynamic_slice_in_dim(padded, margin - relative[0], span, 2)
    tiles = nearby.reshape(nearby.shape[:2] + (2, row_size, local_rows, width))
    tiles = jnp.transpose(tiles, (3, 2, 0, 1, 4, 5)).astype(jnp.bfloat16)
    tiles = jnp.concatenate((tiles, tiles), axis=0)
    outgoing = lax.dynamic_slice_in_dim(tiles, row_size - place, row_size, 0)
    incoming = lax.all_to_all(outgoing, row_axis, 0, 0).astype(jnp.float32)
    same = (chunk_ids <= place)[:, None, None, None, None]
    first = incoming[:, 0]
    second = incoming[:, 1]
    own_rows = jnp.sum(jnp.where(same, first, 0.0), axis=0)
    spills = [
        jnp.sum(jnp.where(same, second, first), axis=0),
        jnp.sum(jnp.where(same, 0.0, second), axis=0),
    ]
    for ahead, spill in zip((1, 2), spills):
        own_rows = own_rows + lax.ppermute(
            spill.astype(jnp.bfloat16),
            tile_axes,
            [(s, (s + ahead * row_size) % tile_count) for s in range(tile_count)],
        ).astype(jnp.float32)
    return jnp.transpose(own_rows, (0, 2, 1, 3))


def row_length(devices):
    places = sorted({device.coords[0] for device in devices})
    return len(places)


def solution(mesh):
    sections, tiles = mesh.devices.shape
    row_size = row_length(list(mesh.devices[0]))
    grid = mesh.devices.reshape(sections, tiles // row_size, row_size)
    grid_mesh = jax.sharding.Mesh(grid, ("section", "lines", "x"))
    tile_axes = ("lines", "x")
    return jax.shard_map(
        functools.partial(on_device, "x", tile_axes),
        mesh=grid_mesh,
        in_specs=(
            P(),
            P(),
            P("section", tile_axes, None, None),
            P(tile_axes),
            P(tile_axes),
            P(tile_axes, None, None),
        ),
        out_specs=P("section", tile_axes, None, None),
        check_vma=False,
    )
```

```python
import functools

import jax
from jax.experimental import pallas as pl
from jax.experimental.pallas import tpu as pltpu
import jax.numpy as jnp
from jax import lax
from jax.sharding import PartitionSpec as P


def shifted(value, axis, steps):
    count = lax.axis_size(axis)
    pairs = [(source, (source + steps) % count) for source in range(count)]
    return lax.ppermute(value, axis, pairs)


def passed_along(shard, axis, by):
    length = lax.axis_size(axis)
    pairs = [(i, i + by) for i in range(length) if 0 <= i + by < length]
    return lax.ppermute(shard, axis, pairs)


def dft_matrix(length):
    points = jnp.arange(length, dtype=jnp.int32)
    product_mod = points[:, None] * points[None, :] % length
    angle = 2.0 * 3.141592653589793 / length * product_mod.astype(jnp.float32)
    scale_fac = 1.0 / jnp.sqrt(jnp.float32(length))
    return jnp.stack((jnp.cos(angle) * scale_fac, -jnp.sin(angle) * scale_fac)).astype(jnp.bfloat16)


def product(form, first, second):
    return jnp.einsum(form, first, second, preferred_element_type=jnp.float32)


def apply_left(matrix, field):
    first_part = product("ij,...jck->...ick", matrix[0], field)
    second_part = product("ij,...jck->...ick", matrix[1], field)
    return jnp.stack(
        (
            first_part[..., 0, :] - second_part[..., 1, :],
            first_part[..., 1, :] + second_part[..., 0, :],
        ),
        axis=-2,
    )


def apply_left_adj(matrix, field):
    first_part = product("ji,...jck->...ick", matrix[0], field)
    second_part = product("ji,...jck->...ick", matrix[1], field)
    return jnp.stack(
        (
            first_part[..., 0, :] + second_part[..., 1, :],
            first_part[..., 1, :] - second_part[..., 0, :],
        ),
        axis=-2,
    )


def apply_right(field, matrix):
    first_part = product("...ick,lk->...icl", field, matrix[0])
    second_part = product("...ick,lk->...icl", field, matrix[1])
    return jnp.stack(
        (
            first_part[..., 0, :] - second_part[..., 1, :],
            second_part[..., 0, :] + first_part[..., 1, :],
        ),
        axis=-2,
    )


def apply_right_conj(field, matrix):
    first_part = product("...ick,kl->...icl", field, matrix[0])
    second_part = product("...ick,kl->...icl", field, matrix[1])
    return jnp.stack(
        (
            first_part[..., 0, :] + second_part[..., 1, :],
            first_part[..., 1, :] - second_part[..., 0, :],
        ),
        axis=-2,
    )


def complex_mul(first, second):
    first = first.astype(jnp.float32)
    second = second.astype(jnp.float32)
    return jnp.stack(
        (
            first[..., 0, :] * second[..., 0, :] - first[..., 1, :] * second[..., 1, :],
            first[..., 0, :] * second[..., 1, :] + first[..., 1, :] * second[..., 0, :],
        ),
        axis=-2,
    )


def conj_mul(first, second):
    first = first.astype(jnp.float32)
    return jnp.stack(
        (
            first[..., 0, :] * second[..., 0, :] + first[..., 1, :] * second[..., 1, :],
            first[..., 0, :] * second[..., 1, :] - first[..., 1, :] * second[..., 0, :],
        ),
        axis=-2,
    )


def accumulate(gradients, starts, buffer_rows):
    width = gradients.shape[-1]
    margin = buffer_rows - width
    placed = jnp.transpose(gradients[0], (1, 0, 2, 3))
    padded = jnp.pad(placed, ((margin, margin), (0, 0), (0, 0), (0, 0)))
    return lax.dynamic_slice_in_dim(padded, margin - starts[0], buffer_rows, 0)


def real_dot(first, second):
    return jnp.dot(first, second, preferred_element_type=jnp.float32)


def times_left(real, imag, field_real, field_imag):
    return (
        real_dot(real, field_real) - real_dot(imag, field_imag),
        real_dot(real, field_imag) + real_dot(imag, field_real),
    )


def times_left_adj(real_t, imag_t, field_real, field_imag):
    return (
        real_dot(real_t, field_real) + real_dot(imag_t, field_imag),
        real_dot(real_t, field_imag) - real_dot(imag_t, field_real),
    )


def times_right(field_real, field_imag, real_t, imag_t):
    return (
        real_dot(field_real, real_t) - real_dot(field_imag, imag_t),
        real_dot(field_real, imag_t) + real_dot(field_imag, real_t),
    )


def times_right_conj(field_real, field_imag, real, imag):
    return (
        real_dot(field_real, real) + real_dot(field_imag, imag),
        real_dot(field_imag, real) - real_dot(field_real, imag),
    )


def rounded(pair):
    return (pair[0].astype(jnp.bfloat16), pair[1].astype(jnp.bfloat16))


def march_steps(field, patch_ref, mats, incident_ref, skip=0):
    real, imag, real_t, imag_t = mats
    field_real, field_imag = field
    for slice_at in range(patch_ref.shape[0]):
        if slice_at >= skip:
            incident_ref[slice_at - skip, 0] = field_real
            incident_ref[slice_at - skip, 1] = field_imag
        first_real = field_real.astype(jnp.float32)
        first_imag = field_imag.astype(jnp.float32)
        second_real = patch_ref[slice_at, 0].astype(jnp.float32)
        second_imag = patch_ref[slice_at, 1].astype(jnp.float32)
        phase = rounded(
            (
                first_real * second_real - first_imag * second_imag,
                first_real * second_imag + first_imag * second_real,
            )
        )
        middle = rounded(times_left(real, imag, *phase))
        field_real, field_imag = rounded(times_right(*middle, real_t, imag_t))
    return (field_real, field_imag)


def far_steps(field, measured, mats):
    real, imag, real_t, imag_t = mats
    half_far = rounded(times_left(real, imag, *field))
    far_real, far_imag = times_right(*half_far, real_t, imag_t)
    misfit = far_real * far_real + far_imag * far_imag - measured.astype(jnp.float32)
    grad_far = rounded((far_real * misfit, far_imag * misfit))
    half_back = rounded(times_left_adj(real_t, imag_t, *grad_far))
    return rounded(times_right_conj(*half_back, real, imag))


def retreat_steps(back, patch_ref, incident_ref, mats, grad_ref, keep_back=True, first=None):
    real, imag, real_t, imag_t = mats
    for slice_at in reversed(range(patch_ref.shape[0])):
        middle = rounded(times_left_adj(real_t, imag_t, *back))
        bar_real, bar_imag = times_right_conj(*middle, real, imag)
        if first is None:
            inc_real = incident_ref[slice_at, 0].astype(jnp.float32)
            inc_imag = incident_ref[slice_at, 1].astype(jnp.float32)
        elif slice_at == 0:
            inc_real = first[0].astype(jnp.float32)
            inc_imag = first[1].astype(jnp.float32)
        else:
            inc_real = incident_ref[slice_at - 1, 0].astype(jnp.float32)
            inc_imag = incident_ref[slice_at - 1, 1].astype(jnp.float32)
        grad_ref[slice_at, 0] = (inc_real * bar_real + inc_imag * bar_imag).astype(grad_ref.dtype)
        grad_ref[slice_at, 1] = (inc_real * bar_imag - inc_imag * bar_real).astype(grad_ref.dtype)
        if slice_at == 0 and not keep_back:
            break
        pat_real = patch_ref[slice_at, 0].astype(jnp.float32)
        pat_imag = patch_ref[slice_at, 1].astype(jnp.float32)
        back = rounded(
            (pat_real * bar_real + pat_imag * bar_imag, pat_real * bar_imag - pat_imag * bar_real)
        )
    return back


def mats_of(mat_ref):
    return (mat_ref[0], mat_ref[1], mat_ref[2], mat_ref[3])


def march_kernel(field_ref, patch_ref, mat_ref, out_ref, incident_ref):
    field = march_steps(
        (field_ref[0], field_ref[1]), patch_ref, mats_of(mat_ref), incident_ref, skip=1
    )
    out_ref[0] = field[0]
    out_ref[1] = field[1]


def middle_kernel(
    field_ref, patch_ref, mat_ref, measured_ref, dft_ref, out_ref, grad_ref, incident_ref
):
    mats = mats_of(mat_ref)
    field = march_steps((field_ref[0], field_ref[1]), patch_ref, mats, incident_ref)
    dft = (dft_ref[0], dft_ref[1], dft_ref[0], dft_ref[1])
    back = far_steps(field, measured_ref[...], dft)
    back = retreat_steps(back, patch_ref, incident_ref, mats, grad_ref)
    out_ref[0] = back[0]
    out_ref[1] = back[1]


def retreat_kernel(back_ref, patch_ref, incident_ref, first_ref, mat_ref, out_ref, grad_ref):
    first = (first_ref[0], first_ref[1])
    back = retreat_steps(
        (back_ref[0], back_ref[1]), patch_ref, incident_ref, mats_of(mat_ref), grad_ref, True, first
    )
    out_ref[0] = back[0]
    out_ref[1] = back[1]


def final_retreat_kernel(back_ref, patch_ref, incident_ref, first_ref, mat_ref, grad_ref):
    first = (first_ref[0], first_ref[1])
    retreat_steps(
        (back_ref[0], back_ref[1]), patch_ref, incident_ref, mats_of(mat_ref), grad_ref, False, first
    )


def planes_of(matrix):
    return jnp.stack((matrix[0], matrix[1], matrix[0].T, matrix[1].T))


def run_kernel(body, outs, flops, *args, scratch=()):
    moved = sum(arg.size * arg.dtype.itemsize for arg in args)
    listed = outs if isinstance(outs, tuple) else (outs,)
    moved += sum(out.size * jnp.dtype(out.dtype).itemsize for out in listed)
    return pl.pallas_call(
        body,
        out_shape=outs,
        scratch_shapes=list(scratch),
        cost_estimate=pl.CostEstimate(flops=flops, transcendentals=0, bytes_accessed=moved),
    )(*args)


def on_device(row_axis, tile_axes, probe, kernel, object_slab, offsets, counts, intensity):
    width = probe.shape[0]
    slot_count = offsets.shape[0]
    local_rows = object_slab.shape[1]
    slice_count = object_slab.shape[0]
    sections = lax.axis_size("section")
    section_now = lax.axis_index("section")
    row_size = lax.axis_size(row_axis)
    tile_count = lax.axis_size(tile_axes)
    tile_now = lax.axis_index(tile_axes)
    place = lax.axis_index(row_axis)
    is_last = section_now == sections - 1
    dft_table = dft_matrix(width)
    chunk_ids = jnp.arange(row_size, dtype=jnp.int32)
    slab = jnp.transpose(object_slab, (0, 2, 1, 3))
    later = [slab] + [
        lax.ppermute(
            slab,
            tile_axes,
            [(s, (s - ahead * row_size) % tile_count) for s in range(tile_count)],
        )
        for ahead in (1, 2)
    ]
    own_row = (chunk_ids <= place)[:, None, None, None, None]
    sent = jnp.stack(
        [jnp.where(own_row, later[half][None], later[half + 1][None]) for half in (0, 1)], axis=1
    )
    got = lax.all_to_all(sent, row_axis, 0, 0)
    got = lax.dynamic_slice_in_dim(jnp.concatenate((got, got), axis=0), place, row_size, 0)
    window = jnp.concatenate(
        [got[at % row_size, at // row_size] for at in range(2 * row_size)], axis=2
    )
    relative = offsets - tile_now * local_rows
    planes = lax.dynamic_slice_in_dim(window, relative[0], width, 2)
    live_slots = jnp.arange(slot_count, dtype=jnp.int32) < counts[0]

    kernel_planes = planes_of(kernel)
    dft_table = dft_matrix(width)
    field_shape = jax.ShapeDtypeStruct((2, width, width), jnp.bfloat16)
    dot_flops = 2 * width**3

    kept_shape = (planes.shape[0] - 1,) + planes.shape[1:]

    def march(field_in):
        outs = (field_shape, jax.ShapeDtypeStruct(kept_shape, jnp.bfloat16))
        flops = slice_count * 8 * dot_flops
        return tuple(run_kernel(march_kernel, outs, flops, field_in, planes, kernel_planes))

    def retreat(back_in, incidents, first):
        outs = (field_shape, jax.ShapeDtypeStruct(planes.shape, jnp.bfloat16))
        flops = slice_count * 8 * dot_flops
        return tuple(
            run_kernel(
                retreat_kernel, outs, flops, back_in, planes, incidents, first, kernel_planes
            )
        )

    def whole(field_in):
        outs = (field_shape, jax.ShapeDtypeStruct(planes.shape, jnp.bfloat16))
        flops = slice_count * 16 * dot_flops + 16 * dot_flops
        scratch = (pltpu.VMEM(planes.shape, jnp.bfloat16),)
        back, grads = run_kernel(
            middle_kernel,
            outs,
            flops,
            field_in,
            planes,
            kernel_planes,
            intensity[0],
            dft_table,
            scratch=scratch,
        )
        return (back, grads)

    stored = jnp.zeros(kept_shape, jnp.bfloat16)
    gradients = jnp.zeros(planes.shape, jnp.bfloat16)
    waves = jnp.transpose(probe, (1, 0, 2))
    entering = waves
    for section_step in range(sections - 1):
        if section_step > 0:
            waves = passed_along(waves, "section", 1)
        waves, stored, entering = lax.cond(
            section_now == section_step,
            lambda field_in, kept, first: march(field_in) + (field_in,),
            lambda field_in, kept, first: (field_in, kept, first),
            waves,
            stored,
            entering,
        )
    waves = passed_along(waves, "section", 1)
    adjoints, gradients = lax.cond(
        is_last,
        lambda field_in, kept: whole(field_in),
        lambda field_in, kept: (field_in, kept),
        waves,
        gradients,
    )
    def final_retreat(back_in, incidents, first):
        outs = jax.ShapeDtypeStruct(planes.shape, jnp.bfloat16)
        flops = planes.shape[0] * 8 * dot_flops
        return run_kernel(
            final_retreat_kernel, outs, flops, back_in, planes, incidents, first, kernel_planes
        )

    for section_step in reversed(range(1, sections - 1)):
        adjoints = passed_along(adjoints, "section", -1)
        adjoints, gradients = lax.cond(
            section_now == section_step,
            lambda field_in, kept: retreat(field_in, stored, entering),
            lambda field_in, kept: (field_in, kept),
            adjoints,
            gradients,
        )
    adjoints = passed_along(adjoints, "section", -1)
    gradients = lax.cond(
        section_now == 0,
        lambda field_in, kept: final_retreat(field_in, stored, entering),
        lambda field_in, kept: kept,
        adjoints,
        gradients,
    )
    gradients = gradients * live_slots[0].astype(jnp.float32)
    span = 2 * row_size * local_rows
    margin = span - width
    padded = jnp.pad(gradients, ((0, 0), (0, 0), (margin, margin), (0, 0)))
    nearby = lax.dynamic_slice_in_dim(padded, margin - relative[0], span, 2)
    tiles = nearby.reshape(nearby.shape[:2] + (2, row_size, local_rows, width))
    tiles = jnp.transpose(tiles, (3, 2, 0, 1, 4, 5)).astype(jnp.bfloat16)
    tiles = jnp.concatenate((tiles, tiles), axis=0)
    outgoing = lax.dynamic_slice_in_dim(tiles, row_size - place, row_size, 0)
    incoming = lax.all_to_all(outgoing, row_axis, 0, 0).astype(jnp.float32)
    same = (chunk_ids <= place)[:, None, None, None, None]
    first = incoming[:, 0]
    second = incoming[:, 1]
    own_rows = jnp.sum(jnp.where(same, first, 0.0), axis=0)
    spills = [
        jnp.sum(jnp.where(same, second, first), axis=0),
        jnp.sum(jnp.where(same, 0.0, second), axis=0),
    ]
    for ahead, spill in zip((1, 2), spills):
        own_rows = own_rows + lax.ppermute(
            spill.astype(jnp.bfloat16),
            tile_axes,
            [(s, (s + ahead * row_size) % tile_count) for s in range(tile_count)],
        ).astype(jnp.float32)
    return jnp.transpose(own_rows, (0, 2, 1, 3))


def row_length(devices):
    places = sorted({device.coords[0] for device in devices})
    return len(places)


def solution(mesh):
    sections, tiles = mesh.devices.shape
    row_size = row_length(list(mesh.devices[0]))
    grid = mesh.devices.reshape(sections, tiles // row_size, row_size)
    grid_mesh = jax.sharding.Mesh(grid, ("section", "lines", "x"))
    tile_axes = ("lines", "x")
    return jax.shard_map(
        functools.partial(on_device, "x", tile_axes),
        mesh=grid_mesh,
        in_specs=(
            P(),
            P(),
            P("section", tile_axes, None, None),
            P(tile_axes),
            P(tile_axes),
            P(tile_axes, None, None),
        ),
        out_specs=P("section", tile_axes, None, None),
        check_vma=False,
    )
```
